768 devices in a mesh: gx: 8 (over x, core), gy: 96 (over z, y).
Axes of the slice: x: 4, y: 8, z: 12, core: 2. Of those that a mesh axis runs over, the one named last changes fastest.
Arguments:
- positions: float32 [3, 196608], P(None, ('gx', 'gy')), may hold values from -1.5 to 1.5
- species: int32 [196608], P(('gx', 'gy')), may hold values from 0 to 3
- neighbours: int32 [1536, 2], P(('gx', 'gy')), may hold values from 0 to 17
- pair_masks: int32 [1536, 2, 128, 128], P(('gx', 'gy')), may hold values 0 or 1
- send_lists: int32 [8, 96, 8, 2], P('gx', 'gy'), may hold values from 0 to 1
- embedding: float32 [4, 64], replicated, may hold values from -6 to 6
- radial: float32 [4, 64], replicated, may hold values from -6 to 6
- readin: float32 [192, 64], replicated, may hold values from -0.4375 to 0.4375
- readout: float32 [64], replicated, may hold values from -0.75 to 0.75
Outputs:
- energies: float32 [196608], P(('gx', 'gy'))
- forces: float32 [3, 196608], P(None, ('gx', 'gy'))
The draws below stay inside these ranges and needn't reach their ends.
Inputs may be any that keep to these rules, and one draw needn't show every extreme that they name: `neighbours`: slot index into the owning device's table of own blocks then ghost blocks. `send_lists`: index of one of the sending device's own blocks.
All inputs are finite; a program needn't handle non-finite values. No bound on the sum of `pair_masks` on one device may be relied on, other than what follows from the above.
Results may differ from the reference program's by a relative error of at most 0.0099.
Values sent between devices are 32-bit elements; how exact they have to be, the bound alone decides.
No kernel may reach another device: no remote copies, remote signals or barrier semaphores. Data moves between devices by JAX's collectives and lax.ppermute only.
A program may use at most 32 MiB of HBM per device.

```python
import math
import jax
import jax.numpy as jnp
from jax import lax

C = 64
RADIAL = 4
SPECIES = 4
BLOCK_ATOMS = 128
NB = 2
G_SEND = 2
B_DEV = 2
BLOCKS = 1536
ATOMS = 196608
N_GX = 8
N_GY = 96


def plant(result, stream_key, least, top_value):
    shape = result.shape
    place = [jax.random.randint(jax.random.fold_in(stream_key, axis), (), 0, shape[axis]) for axis in range(len(shape))]
    result = result.at[tuple(place)].set(least)
    longest = shape.index(max(shape))
    place[longest] = (place[longest] + 1) % shape[longest]
    return result.at[tuple(place)].set(top_value)


def level_of(key, shape, split, least, top_value):
    gain = 1.0
    for position, blocks in split:
        steps = jax.random.uniform(jax.random.fold_in(jax.random.fold_in(key, 6), position), (blocks,), jnp.float32, least / len(split), top_value / len(split))
        gain = gain * jnp.repeat(jnp.exp(steps), shape[position] // blocks).reshape((-1,) + (1,) * (len(shape) - 1 - position))
    return gain


def bell_draw(rng, shape, deviation, limit, held_as=jnp.bfloat16):
    entries = deviation * jax.random.normal(rng, shape, jnp.float32)
    return jnp.clip(entries, min=-limit, max=limit).astype(held_as)


def setup_inputs(seed: int = 0) -> dict:
    arg_keys = jax.random.split(jax.random.key(seed), 10)
    return {
        "positions": jnp.clip(jax.random.uniform(arg_keys[0], (3, ATOMS), jnp.float32, -1.5, 1.5) * level_of(arg_keys[0], (3, ATOMS), ((1, 768),), -0.4, 0.0), -1.5, 1.5),
        "species": plant(jax.random.randint(arg_keys[1], (ATOMS,), 0, SPECIES), jax.random.fold_in(arg_keys[1], 1), 0, SPECIES - 1).astype(jnp.int32),
        "neighbours": plant(jax.random.randint(arg_keys[2], (BLOCKS, NB), 0, B_DEV + 8 * G_SEND), jax.random.fold_in(arg_keys[2], 1), 0, (B_DEV + 8 * G_SEND) - 1).astype(jnp.int32),
        "pair_masks": plant((jax.random.randint(arg_keys[3], (BLOCKS, NB, BLOCK_ATOMS, BLOCK_ATOMS), 0, 2) < 1).astype(jnp.int32), jax.random.fold_in(arg_keys[3], 1), 0, 1),
        "send_lists": plant(jax.random.randint(arg_keys[4], (N_GX, N_GY, 8, G_SEND), 0, B_DEV), jax.random.fold_in(arg_keys[4], 1), 0, B_DEV - 1).astype(jnp.int32),
        "embedding": bell_draw(arg_keys[5], (SPECIES, C), 1.0, 6.0, jnp.float32),
        "radial": bell_draw(arg_keys[6], (RADIAL, C), 1.0, 6.0, jnp.float32),
        "readin": bell_draw(arg_keys[7], (3 * C, C), (3 * C) ** -0.5, 0.4375, jnp.float32),
        "readout": bell_draw(arg_keys[8], (C,), C ** -0.5, 0.75, jnp.float32),
    }


OFFSETS = ((-1, -1), (-1, 0), (-1, 1), (0, -1), (0, 1), (1, -1), (1, 0), (1, 1))
HIGHEST = lax.Precision.HIGHEST

def harmonics(rel, dist):
    ux = rel[0] / dist
    uy = rel[1] / dist
    uz = rel[2] / dist
    root = math.sqrt(3.0)
    return jnp.stack([jnp.ones_like(ux), ux, uy, uz, root * ux * uy, root * uy * uz, root * ux * uz, 0.5 * root * (ux * ux - uy * uy), 0.5 * (3.0 * uz * uz - 1.0)])

def tile_terms(own_pos, other_pos, other_feat, pair_mask, listed):
    atoms = own_pos.shape[1]
    count = RADIAL
    centres = 0.5 + jnp.arange(count).astype(jnp.float32)
    rel = other_pos[:, None, :] - own_pos[:, :, None]
    dist = jnp.sqrt(lax.optimization_barrier(jnp.sum(rel * rel, axis=0)) + 0.25)
    offset = dist[None] - centres[:, None, None]
    basis = jnp.exp(-0.5 * offset * offset)
    angular = harmonics(rel, dist)
    weight = pair_mask.astype(jnp.float32) * (1.0 / math.sqrt(listed * atoms))
    tiles = (basis[:, None] * angular[None] * weight[None, None]).reshape(count * 9, atoms, atoms)
    rounded = lax.optimization_barrier(tiles.astype(jnp.bfloat16))
    return jnp.einsum('qij,cj->qci', rounded.astype(jnp.float32), other_feat.astype(jnp.float32), precision=HIGHEST)

def atom_energy(own_pos, table_pos, table_feat, listed_slots, masks, radial, readin, readout):
    count = radial.shape[0]
    width = table_feat.shape[1]
    atoms = own_pos.shape[1]
    listed = listed_slots.shape[0]
    total = jnp.zeros((count * 9, width, atoms), jnp.float32)
    for slot in range(listed):
        index = listed_slots[slot]
        other_pos = lax.dynamic_index_in_dim(table_pos, index, 0, keepdims=False)
        other_feat = lax.dynamic_index_in_dim(table_feat, index, 0, keepdims=False)
        total = total + tile_terms(own_pos, other_pos, other_feat, masks[slot], listed)
    proj = total.reshape(count, 9, width, atoms)
    message = jnp.einsum('kc,kmci->mci', radial, proj, precision=HIGHEST)
    first = lax.optimization_barrier(jnp.sum(message[1:4] * message[1:4], axis=0))
    second = lax.optimization_barrier(jnp.sum(message[4:9] * message[4:9], axis=0))
    invariants = jnp.concatenate([message[0], first, second], axis=0)
    hidden = jax.nn.silu(jnp.dot(readin.T, invariants, precision=HIGHEST))
    return jnp.dot(readout, hidden, precision=HIGHEST)

def device_terms(own_pos, ghost_pos, own_feat, ghost_feat, listed_slots, masks, radial, readin, readout):

    def energies_of(own_now, ghost_now):
        table_pos = jnp.concatenate([own_now, ghost_now], axis=0)
        table_feat = jnp.concatenate([own_feat, ghost_feat], axis=0)
        return jnp.stack([atom_energy(own_now[block], table_pos, table_feat, listed_slots[block], masks[block], radial, readin, readout) for block in range(own_now.shape[0])])
    energy, pullback = jax.vjp(energies_of, own_pos, ghost_pos)
    grad_own, grad_ghost = pullback(jnp.ones_like(energy))
    return (energy, grad_own, grad_ghost)

def reference(positions, species, neighbours, pair_masks, send_lists, embedding, radial, readin, readout):
    atoms = BLOCK_ATOMS
    onehot = (species[None, :] == jnp.arange(SPECIES).astype(jnp.int32)[:, None]).astype(jnp.float32)
    feats = jnp.dot(embedding.T, onehot, precision=HIGHEST)
    pos_grid = positions.reshape(3, N_GX, N_GY, B_DEV, atoms).transpose(1, 2, 3, 0, 4)
    feat_grid = feats.reshape(C, N_GX, N_GY, B_DEV, atoms).transpose(1, 2, 3, 0, 4).astype(jnp.bfloat16)
    ghost_pos_list = []
    ghost_feat_list = []
    for index, pair in enumerate(OFFSETS):
        chosen = jnp.roll(send_lists[:, :, 7 - index, :], (-pair[0], -pair[1]), (0, 1))
        source_pos = jnp.roll(pos_grid, (-pair[0], -pair[1]), (0, 1))
        source_feat = jnp.roll(feat_grid, (-pair[0], -pair[1]), (0, 1))
        ghost_pos_list.append(jnp.take_along_axis(source_pos, chosen[:, :, :, None, None], axis=2))
        ghost_feat_list.append(jnp.take_along_axis(source_feat, chosen[:, :, :, None, None], axis=2))
    ghost_pos = jnp.concatenate(ghost_pos_list, axis=2)
    ghost_feat = jnp.concatenate(ghost_feat_list, axis=2)
    devices = N_GX * N_GY
    slots = 8 * G_SEND

    def per_device(items):
        return device_terms(items[0], items[1], items[2], items[3], items[4], items[5], radial, readin, readout)
    energy, grad_own, grad_ghost = lax.map(per_device, (pos_grid.reshape(devices, B_DEV, 3, atoms), ghost_pos.reshape(devices, slots, 3, atoms), feat_grid.reshape(devices, B_DEV, C, atoms), ghost_feat.reshape(devices, slots, C, atoms), neighbours.reshape(devices, B_DEV, NB), pair_masks.reshape(devices, B_DEV, NB, atoms, atoms)))
    grad_ghost = grad_ghost.reshape(N_GX, N_GY, 8, G_SEND, 3, atoms)
    returned = jnp.stack([jnp.roll(grad_ghost[:, :, 7 - index], (-pair[0], -pair[1]), (0, 1)) for index, pair in enumerate(OFFSETS)], axis=2)
    pick = (send_lists[..., None] == jnp.arange(B_DEV).astype(jnp.int32)).astype(jnp.float32)
    back = jnp.einsum('xydgb,xydgca->xybca', pick, returned, precision=HIGHEST)
    force_grid = -(grad_own.reshape(N_GX, N_GY, B_DEV, 3, atoms) + back)
    forces = force_grid.transpose(3, 0, 1, 2, 4).reshape(3, ATOMS)
    return (energy.reshape(ATOMS), forces)
```

```python
import math

import jax
import jax.numpy as jnp
from jax import lax
from jax.sharding import PartitionSpec as P

OFFSETS = ((-1, -1), (-1, 0), (-1, 1), (0, -1), (0, 1), (1, -1), (1, 0), (1, 1))
HIGHEST = lax.Precision.HIGHEST


def harmonics(rel, dist):
    ux = rel[0] / dist
    uy = rel[1] / dist
    uz = rel[2] / dist
    root = math.sqrt(3.0)
    return jnp.stack(
        [
            jnp.ones_like(ux),
            ux,
            uy,
            uz,
            root * ux * uy,
            root * uy * uz,
            root * ux * uz,
            0.5 * root * (ux * ux - uy * uy),
            0.5 * (3.0 * uz * uz - 1.0),
        ]
    )


def tile_terms(own_pos, other_pos, other_feat, pair_mask, listed, count):
    atoms = own_pos.shape[1]
    centres = 0.5 + jnp.arange(count).astype(jnp.float32)
    rel = other_pos[:, None, :] - own_pos[:, :, None]
    dist = jnp.sqrt(jnp.sum(rel * rel, axis=0) + 0.25)
    offset = dist[None] - centres[:, None, None]
    basis = jnp.exp(-0.5 * offset * offset)
    angular = harmonics(rel, dist)
    weight = pair_mask.astype(jnp.float32) * (1.0 / math.sqrt(listed * atoms))
    tiles = (basis[:, None] * angular[None] * weight[None, None]).reshape(count * 9, atoms, atoms)
    return jnp.einsum(
        "qij,cj->qci", tiles.astype(jnp.bfloat16), other_feat, preferred_element_type=jnp.float32
    )


def atom_energy(own_pos, table_pos, table_feat, listed_slots, masks, radial, readin, readout):
    count = radial.shape[0]
    width = table_feat.shape[1]
    atoms = own_pos.shape[1]
    listed = listed_slots.shape[0]
    total = jnp.zeros((count * 9, width, atoms), jnp.float32)
    for slot in range(listed):
        index = listed_slots[slot]
        other_pos = lax.dynamic_index_in_dim(table_pos, index, 0, keepdims=False)
        other_feat = lax.dynamic_index_in_dim(table_feat, index, 0, keepdims=False)
        total = total + tile_terms(own_pos, other_pos, other_feat, masks[slot], listed, count)
    proj = total.reshape(count, 9, width, atoms)
    message = jnp.einsum("kc,kmci->mci", radial, proj, precision=HIGHEST)
    first = jnp.sum(message[1:4] * message[1:4], axis=0)
    second = jnp.sum(message[4:9] * message[4:9], axis=0)
    invariants = jnp.concatenate([message[0], first, second], axis=0)
    hidden = jax.nn.silu(jnp.dot(readin.T, invariants, precision=HIGHEST))
    return jnp.dot(readout, hidden, precision=HIGHEST)


def neighbour_shift(x, offset):
    count_x = lax.axis_size("gx")
    count_y = lax.axis_size("gy")
    pairs = []
    for a in range(count_x):
        for b in range(count_y):
            target = ((a + offset[0]) % count_x) * count_y + (b + offset[1]) % count_y
            pairs.append((a * count_y + b, target))
    return lax.ppermute(x, ("gx", "gy"), pairs)


def local(
    positions, species, neighbours, pair_masks, send_lists, embedding, radial, readin, readout
):
    atoms = pair_masks.shape[2]
    blocks = positions.shape[1] // atoms
    kinds = embedding.shape[0]
    sends = send_lists.shape[3]
    own_pos = positions.reshape(3, blocks, atoms).transpose(1, 0, 2)
    own_kind = species.reshape(blocks, 1, atoms).astype(jnp.float32)
    payload = jnp.concatenate([own_pos, own_kind], axis=1)
    chosen = send_lists.reshape(8, sends)
    pick = (chosen[:, :, None] == jnp.arange(blocks)).astype(jnp.float32)
    outgoing = jnp.einsum("dgb,bra->dgra", pick, payload, precision=HIGHEST)
    incoming = jnp.stack(
        [neighbour_shift(outgoing[7 - d], OFFSETS[7 - d]) for d in range(8)], axis=0
    ).reshape(8 * sends, 4, atoms)
    ghost_pos = incoming[:, :3]
    ghost_kind = incoming[:, 3]

    def features(kind):
        onehot = (kind[None, :] == jnp.arange(kinds).astype(kind.dtype)[:, None]).astype(jnp.float32)
        return jnp.dot(embedding.T, onehot, precision=HIGHEST)

    own_feats = features(species)
    own_feat = own_feats.reshape(-1, blocks, atoms).transpose(1, 0, 2).astype(jnp.bfloat16)
    ghost_feat = (
        features(ghost_kind.reshape(-1))
        .reshape(-1, 8 * sends, atoms)
        .transpose(1, 0, 2)
        .astype(jnp.bfloat16)
    )

    def energies_of(own_now, ghost_now):
        table_pos = jnp.concatenate([own_now, ghost_now], axis=0)
        table_feat = jnp.concatenate([own_feat, ghost_feat], axis=0)
        return jnp.stack(
            [
                atom_energy(
                    own_now[block],
                    table_pos,
                    table_feat,
                    neighbours[block],
                    pair_masks[block],
                    radial,
                    readin,
                    readout,
                )
                for block in range(blocks)
            ]
        )

    energy, pullback = jax.vjp(energies_of, own_pos, ghost_pos)
    grad_own, grad_ghost = pullback(jnp.ones_like(energy))
    grad_ghost = grad_ghost.reshape(8, sends, 3, atoms)
    returned = jnp.stack(
        [neighbour_shift(grad_ghost[7 - e], OFFSETS[7 - e]) for e in range(8)], axis=0
    )
    back = jnp.einsum("dgb,dgca->bca", pick, returned, precision=HIGHEST)
    forces = -(grad_own + back)
    return (energy.reshape(blocks * atoms), forces.transpose(1, 0, 2).reshape(3, blocks * atoms))


def solution(mesh):
    placed = (
        P(None, ("gx", "gy")),
        P(("gx", "gy")),
        P(("gx", "gy"), None),
        P(("gx", "gy"), None, None, None),
        P("gx", "gy", None, None),
        P(),
        P(),
        P(),
        P(),
    )
    return jax.shard_map(
        local,
        mesh=mesh,
        in_specs=placed,
        out_specs=(P(("gx", "gy")), P(None, ("gx", "gy"))),
        check_vma=False,
    )
```

```python
import math

import jax
import jax.numpy as jnp
from jax import lax
from jax.sharding import PartitionSpec as P

OFFSETS = ((-1, -1), (-1, 0), (-1, 1), (0, -1), (0, 1), (1, -1), (1, 0), (1, 1))
HIGHEST = lax.Precision.HIGHEST


def harmonics(rel, dist):
    ux = rel[0] / dist
    uy = rel[1] / dist
    uz = rel[2] / dist
    root = math.sqrt(3.0)
    return jnp.stack(
        [
            jnp.ones_like(ux),
            ux,
            uy,
            uz,
            root * ux * uy,
            root * uy * uz,
            root * ux * uz,
            0.5 * root * (ux * ux - uy * uy),
            0.5 * (3.0 * uz * uz - 1.0),
        ]
    )


def tile_terms(own_pos, other_pos, other_feat, pair_mask, listed, count):
    atoms = own_pos.shape[1]
    centres = 0.5 + jnp.arange(count).astype(jnp.float32)
    rel = other_pos[:, None, :] - own_pos[:, :, None]
    dist = jnp.sqrt(jnp.sum(rel * rel, axis=0) + 0.25)
    offset = dist[None] - centres[:, None, None]
    basis = jnp.exp(-0.5 * offset * offset)
    angular = harmonics(rel, dist)
    weight = pair_mask.astype(jnp.float32) * (1.0 / math.sqrt(listed * atoms))
    tiles = (basis[:, None] * angular[None] * weight[None, None]).reshape(count * 9, atoms, atoms)
    return jnp.einsum(
        "qij,cj->qci", tiles.astype(jnp.bfloat16), other_feat, preferred_element_type=jnp.float32
    )


def atom_energy(own_pos, table_pos, table_feat, listed_slots, masks, radial, readin, readout):
    count = radial.shape[0]
    width = table_feat.shape[1]
    atoms = own_pos.shape[1]
    listed = listed_slots.shape[0]
    total = jnp.zeros((count * 9, width, atoms), jnp.float32)
    for slot in range(listed):
        index = listed_slots[slot]
        other_pos = lax.dynamic_index_in_dim(table_pos, index, 0, keepdims=False)
        other_feat = lax.dynamic_index_in_dim(table_feat, index, 0, keepdims=False)
        total = total + tile_terms(own_pos, other_pos, other_feat, masks[slot], listed, count)
    proj = total.reshape(count, 9, width, atoms)
    message = jnp.einsum("kc,kmci->mci", radial, proj, precision=HIGHEST)
    first = jnp.sum(message[1:4] * message[1:4], axis=0)
    second = jnp.sum(message[4:9] * message[4:9], axis=0)
    invariants = jnp.concatenate([message[0], first, second], axis=0)
    hidden = jax.nn.silu(jnp.dot(readin.T, invariants, precision=HIGHEST))
    return jnp.dot(readout, hidden, precision=HIGHEST)


def halo(grid):
    count_x = lax.axis_size("gx")
    count_y = lax.axis_size("gy")
    up_x = [(i, (i + 1) % count_x) for i in range(count_x)]
    down_x = [((i + 1) % count_x, i) for i in range(count_x)]
    up_y = [(i, (i + 1) % count_y) for i in range(count_y)]
    down_y = [((i + 1) % count_y, i) for i in range(count_y)]
    from_left_x = lax.ppermute(grid[2], "gx", up_x)
    from_right_x = lax.ppermute(grid[0], "gx", down_x)
    rows = jnp.stack([from_left_x, grid[1], from_right_x], axis=0)
    from_left_y = lax.ppermute(rows[:, 2], "gy", up_y)
    from_right_y = lax.ppermute(rows[:, 0], "gy", down_y)
    return jnp.stack([from_left_y, rows[:, 1], from_right_y], axis=1)


def place(parts):
    empty = jnp.zeros_like(parts[0:1])
    full = jnp.concatenate([parts[:4], empty, parts[4:]], axis=0)
    return full.reshape((3, 3) + parts.shape[1:])


def collect(grid):
    return jnp.stack([grid[1 + pair[0], 1 + pair[1]] for pair in OFFSETS], axis=0)


def local(
    positions, species, neighbours, pair_masks, send_lists, embedding, radial, readin, readout
):
    atoms = pair_masks.shape[2]
    blocks = positions.shape[1] // atoms
    kinds = embedding.shape[0]
    sends = send_lists.shape[3]
    own_pos = positions.reshape(3, blocks, atoms).transpose(1, 0, 2)
    own_kind = species.reshape(blocks, 1, atoms).astype(jnp.float32)
    payload = jnp.concatenate([own_pos, own_kind], axis=1)
    chosen = send_lists.reshape(8, sends)
    pick = (chosen[:, :, None] == jnp.arange(blocks)).astype(jnp.float32)
    outgoing = jnp.einsum("dgb,bra->dgra", pick, payload, precision=HIGHEST)
    incoming = collect(halo(place(outgoing))).reshape(8 * sends, 4, atoms)
    ghost_pos = incoming[:, :3]
    ghost_kind = incoming[:, 3]

    def features(kind):
        onehot = (kind[None, :] == jnp.arange(kinds).astype(kind.dtype)[:, None]).astype(jnp.float32)
        return jnp.dot(embedding.T, onehot, precision=HIGHEST)

    own_feats = features(species)
    own_feat = own_feats.reshape(-1, blocks, atoms).transpose(1, 0, 2).astype(jnp.bfloat16)
    ghost_feat = (
        features(ghost_kind.reshape(-1))
        .reshape(-1, 8 * sends, atoms)
        .transpose(1, 0, 2)
        .astype(jnp.bfloat16)
    )

    def energies_of(own_now, ghost_now):
        table_pos = jnp.concatenate([own_now, ghost_now], axis=0)
        table_feat = jnp.concatenate([own_feat, ghost_feat], axis=0)
        return jnp.stack(
            [
                atom_energy(
                    own_now[block],
                    table_pos,
                    table_feat,
                    neighbours[block],
                    pair_masks[block],
                    radial,
                    readin,
                    readout,
                )
                for block in range(blocks)
            ]
        )

    energy, pullback = jax.vjp(energies_of, own_pos, ghost_pos)
    grad_own, grad_ghost = pullback(jnp.ones_like(energy))
    returned = collect(halo(place(grad_ghost.reshape(8, sends, 3, atoms))))
    back = jnp.einsum("dgb,dgca->bca", pick, returned, precision=HIGHEST)
    forces = -(grad_own + back)
    return (energy.reshape(blocks * atoms), forces.transpose(1, 0, 2).reshape(3, blocks * atoms))


def solution(mesh):
    placed = (
        P(None, ("gx", "gy")),
        P(("gx", "gy")),
        P(("gx", "gy"), None),
        P(("gx", "gy"), None, None, None),
        P("gx", "gy", None, None),
        P(),
        P(),
        P(),
        P(),
    )
    return jax.shard_map(
        local,
        mesh=mesh,
        in_specs=placed,
        out_specs=(P(("gx", "gy")), P(None, ("gx", "gy"))),
        check_vma=False,
    )
```

```python
import math

import jax
import jax.numpy as jnp
from jax import lax
from jax.sharding import PartitionSpec as P

OFFSETS = ((-1, -1), (-1, 0), (-1, 1), (0, -1), (0, 1), (1, -1), (1, 0), (1, 1))
HIGHEST = lax.Precision.HIGHEST


def harmonics(rel, dist):
    ux = rel[0] / dist
    uy = rel[1] / dist
    uz = rel[2] / dist
    root = math.sqrt(3.0)
    return jnp.stack(
        [
            jnp.ones_like(ux),
            ux,
            uy,
            uz,
            root * ux * uy,
            root * uy * uz,
            root * ux * uz,
            0.5 * root * (ux * ux - uy * uy),
            0.5 * (3.0 * uz * uz - 1.0),
        ]
    )


def tile_terms(own_pos, other_pos, other_feat, pair_mask, listed, count):
    atoms = own_pos.shape[1]
    centres = 0.5 + jnp.arange(count).astype(jnp.float32)
    rel = other_pos[:, None, :] - own_pos[:, :, None]
    dist = jnp.sqrt(jnp.sum(rel * rel, axis=0) + 0.25)
    offset = dist[None] - centres[:, None, None]
    basis = jnp.exp(-0.5 * offset * offset)
    angular = harmonics(rel, dist)
    weight = pair_mask.astype(jnp.float32) * (1.0 / math.sqrt(listed * atoms))
    tiles = (basis[:, None] * angular[None] * weight[None, None]).reshape(count * 9, atoms, atoms)
    return jnp.einsum(
        "qij,cj->qci", tiles.astype(jnp.bfloat16), other_feat, preferred_element_type=jnp.float32
    )


def atom_energy(own_pos, others_pos, others_feat, masks, radial, readin, readout):
    count = radial.shape[0]
    width = others_feat.shape[1]
    atoms = own_pos.shape[1]
    listed = others_pos.shape[0]
    total = jnp.zeros((count * 9, width, atoms), jnp.float32)
    for slot in range(listed):
        total = total + tile_terms(
            own_pos, others_pos[slot], others_feat[slot], masks[slot], listed, count
        )
    proj = total.reshape(count, 9, width, atoms)
    message = jnp.sum(radial[:, None, :, None] * proj, axis=0)
    first = jnp.sum(message[1:4] * message[1:4], axis=0)
    second = jnp.sum(message[4:9] * message[4:9], axis=0)
    invariants = jnp.concatenate([message[0], first, second], axis=0)
    hidden = jax.nn.silu(jnp.dot(readin.T, invariants, precision=HIGHEST))
    return jnp.dot(readout, hidden, precision=HIGHEST)


def select_slots(table, chosen):
    slots = table.shape[0]
    hit = chosen[..., None] == jnp.arange(slots, dtype=chosen.dtype)
    hit = hit.reshape(hit.shape + (1,) * (table.ndim - 1))
    return jnp.sum(jnp.where(hit, table, jnp.zeros((), table.dtype)), axis=2)


def halo(grid):
    count_x = lax.axis_size("gx")
    count_y = lax.axis_size("gy")
    up_x = [(i, (i + 1) % count_x) for i in range(count_x)]
    down_x = [((i + 1) % count_x, i) for i in range(count_x)]
    up_y = [(i, (i + 1) % count_y) for i in range(count_y)]
    down_y = [((i + 1) % count_y, i) for i in range(count_y)]
    from_left_x = lax.ppermute(grid[2], "gx", up_x)
    from_right_x = lax.ppermute(grid[0], "gx", down_x)
    rows = jnp.stack([from_left_x, grid[1], from_right_x], axis=0)
    from_left_y = lax.ppermute(rows[:, 2], "gy", up_y)
    from_right_y = lax.ppermute(rows[:, 0], "gy", down_y)
    return jnp.stack([from_left_y, rows[:, 1], from_right_y], axis=1)


def place(parts):
    empty = jnp.zeros_like(parts[0:1])
    full = jnp.concatenate([parts[:4], empty, parts[4:]], axis=0)
    return full.reshape((3, 3) + parts.shape[1:])


def collect(grid):
    return jnp.stack([grid[1 + pair[0], 1 + pair[1]] for pair in OFFSETS], axis=0)


def local(
    positions, species, neighbours, pair_masks, send_lists, embedding, radial, readin, readout
):
    atoms = pair_masks.shape[2]
    blocks = positions.shape[1] // atoms
    kinds = embedding.shape[0]
    sends = send_lists.shape[3]
    own_pos = positions.reshape(3, blocks, atoms).transpose(1, 0, 2)
    own_kind = species.reshape(blocks, 1, atoms).astype(jnp.float32)
    payload = jnp.concatenate([own_pos, own_kind], axis=1)
    chosen = send_lists.reshape(8, sends)
    pick = (chosen[:, :, None] == jnp.arange(blocks)).astype(jnp.float32)
    outgoing = jnp.einsum("dgb,bra->dgra", pick, payload, precision=HIGHEST)
    incoming = collect(halo(place(outgoing))).reshape(8 * sends, 4, atoms)
    ghost_pos = incoming[:, :3]
    ghost_kind = incoming[:, 3]

    def features(kind):
        onehot = (kind[None, :] == jnp.arange(kinds).astype(kind.dtype)[:, None]).astype(jnp.float32)
        return jnp.dot(embedding.T, onehot, precision=HIGHEST)

    own_feats32 = features(species).reshape(-1, blocks, atoms).transpose(1, 0, 2)
    ghost_feats32 = (
        features(ghost_kind.reshape(-1)).reshape(-1, 8 * sends, atoms).transpose(1, 0, 2)
    )

    def energies_of(own_now, ghost_now):
        table_pos = jnp.concatenate([own_now, ghost_now], axis=0)
        table_feat = jnp.concatenate([own_feats32, ghost_feats32], axis=0)
        others_pos = select_slots(table_pos, neighbours)
        others_feat = select_slots(table_feat, neighbours).astype(jnp.bfloat16)
        return jnp.stack(
            [
                atom_energy(
                    own_now[block],
                    others_pos[block],
                    others_feat[block],
                    pair_masks[block],
                    radial,
                    readin,
                    readout,
                )
                for block in range(blocks)
            ]
        )

    energy, pullback = jax.vjp(energies_of, own_pos, ghost_pos)
    grad_own, grad_ghost = pullback(jnp.ones_like(energy))
    returned = collect(halo(place(grad_ghost.reshape(8, sends, 3, atoms))))
    back = jnp.einsum("dgb,dgca->bca", pick, returned, precision=HIGHEST)
    forces = -(grad_own + back)
    return (energy.reshape(blocks * atoms), forces.transpose(1, 0, 2).reshape(3, blocks * atoms))


def solution(mesh):
    placed = (
        P(None, ("gx", "gy")),
        P(("gx", "gy")),
        P(("gx", "gy"), None),
        P(("gx", "gy"), None, None, None),
        P("gx", "gy", None, None),
        P(),
        P(),
        P(),
        P(),
    )
    return jax.shard_map(
        local,
        mesh=mesh,
        in_specs=placed,
        out_specs=(P(("gx", "gy")), P(None, ("gx", "gy"))),
        check_vma=False,
    )
```

```python
import math

import jax
import jax.numpy as jnp
from jax import lax
from jax.sharding import PartitionSpec as P

OFFSETS = ((-1, -1), (-1, 0), (-1, 1), (0, -1), (0, 1), (1, -1), (1, 0), (1, 1))
HIGHEST = lax.Precision.HIGHEST


def harmonics(rel, dist):
    ux = rel[0] / dist
    uy = rel[1] / dist
    uz = rel[2] / dist
    root = math.sqrt(3.0)
    return jnp.stack(
        [
            jnp.ones_like(ux),
            ux,
            uy,
            uz,
            root * ux * uy,
            root * uy * uz,
            root * ux * uz,
            0.5 * root * (ux * ux - uy * uy),
            0.5 * (3.0 * uz * uz - 1.0),
        ]
    )


def block_energies(own_pos, others_pos, others_feat, masks, radial, readin, readout):
    count = radial.shape[0]
    atoms = own_pos.shape[2]
    listed = others_pos.shape[1]
    centres = 0.5 + jnp.arange(count).astype(jnp.float32)
    rel = others_pos[:, :, :, None, :] - own_pos[:, None, :, :, None]
    dist = jnp.sqrt(jnp.sum(rel * rel, axis=2) + 0.25)
    offset = dist[:, :, None] - centres[:, None, None]
    basis = jnp.exp(-0.5 * offset * offset)
    angular = harmonics(jnp.moveaxis(rel, 2, 0), dist)
    angular = jnp.moveaxis(angular, 0, 2)
    weight = masks.astype(jnp.float32) * (1.0 / math.sqrt(listed * atoms))
    tiles = basis[:, :, :, None] * angular[:, :, None] * weight[:, :, None, None]
    tiles = tiles.reshape(tiles.shape[:2] + (count * 9, atoms, atoms)).astype(jnp.bfloat16)
    proj = jnp.einsum("bnqij,bncj->bqci", tiles, others_feat, preferred_element_type=jnp.float32)
    proj = proj.reshape((proj.shape[0], count, 9) + proj.shape[2:])
    message = jnp.sum(radial[None, :, None, :, None] * proj, axis=1)
    first = jnp.sum(message[:, 1:4] * message[:, 1:4], axis=1)
    second = jnp.sum(message[:, 4:9] * message[:, 4:9], axis=1)
    invariants = jnp.concatenate([message[:, 0], first, second], axis=1)
    hidden = jax.nn.silu(jnp.einsum("fh,bfi->bhi", readin, invariants, precision=HIGHEST))
    return jnp.einsum("h,bhi->bi", readout, hidden, precision=HIGHEST)


def select_slots(table, chosen):
    slots = table.shape[0]
    hit = chosen[..., None] == jnp.arange(slots, dtype=chosen.dtype)
    hit = hit.reshape(hit.shape + (1,) * (table.ndim - 1))
    return jnp.sum(jnp.where(hit, table, jnp.zeros((), table.dtype)), axis=2)


def halo(grid):
    count_x = lax.axis_size("gx")
    count_y = lax.axis_size("gy")
    up_x = [(i, (i + 1) % count_x) for i in range(count_x)]
    down_x = [((i + 1) % count_x, i) for i in range(count_x)]
    up_y = [(i, (i + 1) % count_y) for i in range(count_y)]
    down_y = [((i + 1) % count_y, i) for i in range(count_y)]
    from_left_x = lax.ppermute(grid[2], "gx", up_x)
    from_right_x = lax.ppermute(grid[0], "gx", down_x)
    rows = jnp.stack([from_left_x, grid[1], from_right_x], axis=0)
    from_left_y = lax.ppermute(rows[:, 2], "gy", up_y)
    from_right_y = lax.ppermute(rows[:, 0], "gy", down_y)
    return jnp.stack([from_left_y, rows[:, 1], from_right_y], axis=1)


def place(parts):
    empty = jnp.zeros_like(parts[0:1])
    full = jnp.concatenate([parts[:4], empty, parts[4:]], axis=0)
    return full.reshape((3, 3) + parts.shape[1:])


def collect(grid):
    return jnp.stack([grid[1 + pair[0], 1 + pair[1]] for pair in OFFSETS], axis=0)


def local(
    positions, species, neighbours, pair_masks, send_lists, embedding, radial, readin, readout
):
    atoms = pair_masks.shape[2]
    blocks = positions.shape[1] // atoms
    kinds = embedding.shape[0]
    sends = send_lists.shape[3]
    own_pos = positions.reshape(3, blocks, atoms).transpose(1, 0, 2)
    own_kind = species.reshape(blocks, 1, atoms).astype(jnp.float32)
    payload = jnp.concatenate([own_pos, own_kind], axis=1)
    chosen = send_lists.reshape(8, sends)
    pick = (chosen[:, :, None] == jnp.arange(blocks)).astype(jnp.float32)
    outgoing = jnp.einsum("dgb,bra->dgra", pick, payload, precision=HIGHEST)
    incoming = collect(halo(place(outgoing))).reshape(8 * sends, 4, atoms)
    ghost_pos = incoming[:, :3]
    ghost_kind = incoming[:, 3]

    def features(kind):
        onehot = (kind[None, :] == jnp.arange(kinds).astype(kind.dtype)[:, None]).astype(jnp.float32)
        return jnp.dot(embedding.T, onehot, precision=HIGHEST)

    own_feats32 = features(species).reshape(-1, blocks, atoms).transpose(1, 0, 2)
    ghost_feats32 = (
        features(ghost_kind.reshape(-1)).reshape(-1, 8 * sends, atoms).transpose(1, 0, 2)
    )

    def energies_of(own_now, ghost_now):
        table_pos = jnp.concatenate([own_now, ghost_now], axis=0)
        table_feat = jnp.concatenate([own_feats32, ghost_feats32], axis=0)
        others_pos = select_slots(table_pos, neighbours)
        others_feat = select_slots(table_feat, neighbours).astype(jnp.bfloat16)
        return block_energies(
            own_now, others_pos, others_feat, pair_masks, radial, readin, readout
        )

    energy, pullback = jax.vjp(energies_of, own_pos, ghost_pos)
    grad_own, grad_ghost = pullback(jnp.ones_like(energy))
    returned = collect(halo(place(grad_ghost.reshape(8, sends, 3, atoms))))
    back = jnp.einsum("dgb,dgca->bca", pick, returned, precision=HIGHEST)
    forces = -(grad_own + back)
    return (energy.reshape(blocks * atoms), forces.transpose(1, 0, 2).reshape(3, blocks * atoms))


def solution(mesh):
    placed = (
        P(None, ("gx", "gy")),
        P(("gx", "gy")),
        P(("gx", "gy"), None),
        P(("gx", "gy"), None, None, None),
        P("gx", "gy", None, None),
        P(),
        P(),
        P(),
        P(),
    )
    return jax.shard_map(
        local,
        mesh=mesh,
        in_specs=placed,
        out_specs=(P(("gx", "gy")), P(None, ("gx", "gy"))),
        check_vma=False,
    )
```

```python
import math

import jax
import jax.numpy as jnp
from jax import lax
from jax.sharding import PartitionSpec as P

OFFSETS = ((-1, -1), (-1, 0), (-1, 1), (0, -1), (0, 1), (1, -1), (1, 0), (1, 1))
HIGHEST = lax.Precision.HIGHEST


def harmonics(rel, dist):
    ux = rel[0] / dist
    uy = rel[1] / dist
    uz = rel[2] / dist
    root = math.sqrt(3.0)
    return jnp.stack(
        [
            jnp.ones_like(ux),
            ux,
            uy,
            uz,
            root * ux * uy,
            root * uy * uz,
            root * ux * uz,
            0.5 * root * (ux * ux - uy * uy),
            0.5 * (3.0 * uz * uz - 1.0),
        ]
    )


def block_energies(own_pos, others_pos, others_feat, masks, radial, readin, readout):
    count = radial.shape[0]
    atoms = own_pos.shape[2]
    listed = others_pos.shape[2] // atoms
    centres = 0.5 + jnp.arange(count).astype(jnp.float32)
    rel = others_pos[:, :, None, :] - own_pos[:, :, :, None]
    dist = jnp.sqrt(jnp.sum(rel * rel, axis=1) + 0.25)
    offset = dist[:, None] - centres[:, None, None]
    basis = jnp.exp(-0.5 * offset * offset)
    angular = jnp.moveaxis(harmonics(jnp.moveaxis(rel, 1, 0), dist), 0, 1)
    weight = masks.astype(jnp.float32) * (1.0 / math.sqrt(listed * atoms))
    tiles = basis[:, :, None] * angular[:, None] * weight[:, None, None]
    tiles = tiles.reshape((tiles.shape[0], count * 9) + tiles.shape[3:]).astype(jnp.bfloat16)
    proj = jnp.einsum("bqij,bcj->bqci", tiles, others_feat, preferred_element_type=jnp.float32)
    proj = proj.reshape((proj.shape[0], count, 9) + proj.shape[2:])
    message = jnp.sum(radial[None, :, None, :, None] * proj, axis=1)
    first = jnp.sum(message[:, 1:4] * message[:, 1:4], axis=1)
    second = jnp.sum(message[:, 4:9] * message[:, 4:9], axis=1)
    invariants = jnp.concatenate([message[:, 0], first, second], axis=1)
    hidden = jax.nn.silu(jnp.einsum("fh,bfi->bhi", readin, invariants, precision=HIGHEST))
    return jnp.einsum("h,bhi->bi", readout, hidden, precision=HIGHEST)


def end_to_end(x):
    return jnp.swapaxes(x, 1, 2).reshape(x.shape[0], x.shape[2], x.shape[1] * x.shape[3])


def select_slots(table, chosen):
    slots = table.shape[0]
    hit = chosen[..., None] == jnp.arange(slots, dtype=chosen.dtype)
    hit = hit.reshape(hit.shape + (1,) * (table.ndim - 1))
    return jnp.sum(jnp.where(hit, table, jnp.zeros((), table.dtype)), axis=2)


def halo(grid):
    count_x = lax.axis_size("gx")
    count_y = lax.axis_size("gy")
    up_x = [(i, (i + 1) % count_x) for i in range(count_x)]
    down_x = [((i + 1) % count_x, i) for i in range(count_x)]
    up_y = [(i, (i + 1) % count_y) for i in range(count_y)]
    down_y = [((i + 1) % count_y, i) for i in range(count_y)]
    from_left_x = lax.ppermute(grid[2], "gx", up_x)
    from_right_x = lax.ppermute(grid[0], "gx", down_x)
    rows = jnp.stack([from_left_x, grid[1], from_right_x], axis=0)
    from_left_y = lax.ppermute(rows[:, 2], "gy", up_y)
    from_right_y = lax.ppermute(rows[:, 0], "gy", down_y)
    return jnp.stack([from_left_y, rows[:, 1], from_right_y], axis=1)


def place(parts):
    empty = jnp.zeros_like(parts[0:1])
    full = jnp.concatenate([parts[:4], empty, parts[4:]], axis=0)
    return full.reshape((3, 3) + parts.shape[1:])


def collect(grid):
    return jnp.stack([grid[1 + pair[0], 1 + pair[1]] for pair in OFFSETS], axis=0)


def local(
    positions, species, neighbours, pair_masks, send_lists, embedding, radial, readin, readout
):
    atoms = pair_masks.shape[2]
    blocks = positions.shape[1] // atoms
    kinds = embedding.shape[0]
    sends = send_lists.shape[3]
    own_pos = positions.reshape(3, blocks, atoms).transpose(1, 0, 2)
    own_kind = species.reshape(blocks, 1, atoms).astype(jnp.float32)
    payload = jnp.concatenate([own_pos, own_kind], axis=1)
    chosen = send_lists.reshape(8, sends)
    pick = (chosen[:, :, None] == jnp.arange(blocks)).astype(jnp.float32)
    outgoing = jnp.einsum("dgb,bra->dgra", pick, payload, precision=HIGHEST)
    incoming = collect(halo(place(outgoing))).reshape(8 * sends, 4, atoms)
    ghost_pos = incoming[:, :3]
    ghost_kind = incoming[:, 3]

    def features(kind):
        onehot = (kind[None, :] == jnp.arange(kinds).astype(kind.dtype)[:, None]).astype(jnp.float32)
        return jnp.dot(embedding.T, onehot, precision=HIGHEST)

    own_feats32 = features(species).reshape(-1, blocks, atoms).transpose(1, 0, 2)
    ghost_feats32 = (
        features(ghost_kind.reshape(-1)).reshape(-1, 8 * sends, atoms).transpose(1, 0, 2)
    )

    masks_joined = end_to_end(pair_masks)

    def energies_of(own_now, ghost_now):
        table_pos = jnp.concatenate([own_now, ghost_now], axis=0)
        table_feat = jnp.concatenate([own_feats32, ghost_feats32], axis=0)
        others_pos = end_to_end(select_slots(table_pos, neighbours))
        others_feat = end_to_end(select_slots(table_feat, neighbours).astype(jnp.bfloat16))
        return block_energies(own_now, others_pos, others_feat, masks_joined, radial, readin, readout)

    energy, pullback = jax.vjp(energies_of, own_pos, ghost_pos)
    grad_own, grad_ghost = pullback(jnp.ones_like(energy))
    returned = collect(halo(place(grad_ghost.reshape(8, sends, 3, atoms))))
    back = jnp.einsum("dgb,dgca->bca", pick, returned, precision=HIGHEST)
    forces = -(grad_own + back)
    return (energy.reshape(blocks * atoms), forces.transpose(1, 0, 2).reshape(3, blocks * atoms))


def solution(mesh):
    placed = (
        P(None, ("gx", "gy")),
        P(("gx", "gy")),
        P(("gx", "gy"), None),
        P(("gx", "gy"), None, None, None),
        P("gx", "gy", None, None),
        P(),
        P(),
        P(),
        P(),
    )
    return jax.shard_map(
        local,
        mesh=mesh,
        in_specs=placed,
        out_specs=(P(("gx", "gy")), P(None, ("gx", "gy"))),
        check_vma=False,
    )
```

```python
import math

import jax
import jax.numpy as jnp
from jax import lax
from jax.sharding import PartitionSpec as P

OFFSETS = ((-1, -1), (-1, 0), (-1, 1), (0, -1), (0, 1), (1, -1), (1, 0), (1, 1))
HIGHEST = lax.Precision.HIGHEST


def harmonics(rel, dist):
    ux = rel[0] / dist
    uy = rel[1] / dist
    uz = rel[2] / dist
    root = math.sqrt(3.0)
    return jnp.stack(
        [
            jnp.ones_like(ux),
            ux,
            uy,
            uz,
            root * ux * uy,
            root * uy * uz,
            root * ux * uz,
            0.5 * root * (ux * ux - uy * uy),
            0.5 * (3.0 * uz * uz - 1.0),
        ]
    )


def tile_terms(own_pos, other_pos, other_feat, pair_mask, listed, count):
    atoms = own_pos.shape[1]
    centres = 0.5 + jnp.arange(count).astype(jnp.float32)
    rel = other_pos[:, None, :] - own_pos[:, :, None]
    dist = jnp.sqrt(jnp.sum(rel * rel, axis=0) + 0.25)
    offset = dist[None] - centres[:, None, None]
    basis = jnp.exp(-0.5 * offset * offset)
    angular = harmonics(rel, dist)
    weight = pair_mask.astype(jnp.float32) * (1.0 / math.sqrt(listed * atoms))
    tiles = (basis[:, None] * angular[None] * weight[None, None]).reshape(count * 9, atoms, atoms)
    return jnp.einsum(
        "qij,cj->qic", tiles.astype(jnp.bfloat16), other_feat, preferred_element_type=jnp.float32
    )


def atom_energy(own_pos, others_pos, others_feat, masks, radial, readin, readout):
    count = radial.shape[0]
    width = others_feat.shape[1]
    atoms = own_pos.shape[1]
    listed = others_pos.shape[0]
    total = jnp.zeros((count * 9, atoms, width), jnp.float32)
    for slot in range(listed):
        total = total + tile_terms(
            own_pos, others_pos[slot], others_feat[slot], masks[slot], listed, count
        )
    proj = total.reshape(count, 9, atoms, width)
    message = jnp.sum(radial[:, None, None, :] * proj, axis=0)
    first = jnp.sum(message[1:4] * message[1:4], axis=0)
    second = jnp.sum(message[4:9] * message[4:9], axis=0)
    invariants = jnp.concatenate([message[0], first, second], axis=1)
    hidden = jax.nn.silu(jnp.dot(invariants, readin, precision=HIGHEST))
    return jnp.dot(hidden, readout, precision=HIGHEST)


def select_slots(table, chosen):
    slots = table.shape[0]
    hit = chosen[..., None] == jnp.arange(slots, dtype=chosen.dtype)
    hit = hit.reshape(hit.shape + (1,) * (table.ndim - 1))
    return jnp.sum(jnp.where(hit, table, jnp.zeros((), table.dtype)), axis=2)


def halo(grid):
    count_x = lax.axis_size("gx")
    count_y = lax.axis_size("gy")
    up_x = [(i, (i + 1) % count_x) for i in range(count_x)]
    down_x = [((i + 1) % count_x, i) for i in range(count_x)]
    up_y = [(i, (i + 1) % count_y) for i in range(count_y)]
    down_y = [((i + 1) % count_y, i) for i in range(count_y)]
    from_left_x = lax.ppermute(grid[2], "gx", up_x)
    from_right_x = lax.ppermute(grid[0], "gx", down_x)
    rows = jnp.stack([from_left_x, grid[1], from_right_x], axis=0)
    from_left_y = lax.ppermute(rows[:, 2], "gy", up_y)
    from_right_y = lax.ppermute(rows[:, 0], "gy", down_y)
    return jnp.stack([from_left_y, rows[:, 1], from_right_y], axis=1)


def place(parts):
    empty = jnp.zeros_like(parts[0:1])
    full = jnp.concatenate([parts[:4], empty, parts[4:]], axis=0)
    return full.reshape((3, 3) + parts.shape[1:])


def collect(grid):
    return jnp.stack([grid[1 + pair[0], 1 + pair[1]] for pair in OFFSETS], axis=0)


def local(
    positions, species, neighbours, pair_masks, send_lists, embedding, radial, readin, readout
):
    atoms = pair_masks.shape[2]
    blocks = positions.shape[1] // atoms
    kinds = embedding.shape[0]
    sends = send_lists.shape[3]
    own_pos = positions.reshape(3, blocks, atoms).transpose(1, 0, 2)
    own_kind = species.reshape(blocks, 1, atoms).astype(jnp.float32)
    payload = jnp.concatenate([own_pos, own_kind], axis=1)
    chosen = send_lists.reshape(8, sends)
    pick = (chosen[:, :, None] == jnp.arange(blocks)).astype(jnp.float32)
    outgoing = jnp.einsum("dgb,bra->dgra", pick, payload, precision=HIGHEST)
    incoming = collect(halo(place(outgoing))).reshape(8 * sends, 4, atoms)
    ghost_pos = incoming[:, :3]
    ghost_kind = incoming[:, 3]

    def features(kind):
        onehot = (kind[None, :] == jnp.arange(kinds).astype(kind.dtype)[:, None]).astype(jnp.float32)
        return jnp.dot(embedding.T, onehot, precision=HIGHEST)

    own_feats32 = features(species).reshape(-1, blocks, atoms).transpose(1, 0, 2)
    ghost_feats32 = (
        features(ghost_kind.reshape(-1)).reshape(-1, 8 * sends, atoms).transpose(1, 0, 2)
    )

    def energies_of(own_now, ghost_now):
        table_pos = jnp.concatenate([own_now, ghost_now], axis=0)
        table_feat = jnp.concatenate([own_feats32, ghost_feats32], axis=0)
        others_pos = select_slots(table_pos, neighbours)
        others_feat = select_slots(table_feat, neighbours).astype(jnp.bfloat16)
        return jnp.stack(
            [
                atom_energy(
                    own_now[block],
                    others_pos[block],
                    others_feat[block],
                    pair_masks[block],
                    radial,
                    readin,
                    readout,
                )
                for block in range(blocks)
            ]
        )

    energy, pullback = jax.vjp(energies_of, own_pos, ghost_pos)
    grad_own, grad_ghost = pullback(jnp.ones_like(energy))
    returned = collect(halo(place(grad_ghost.reshape(8, sends, 3, atoms))))
    back = jnp.einsum("dgb,dgca->bca", pick, returned, precision=HIGHEST)
    forces = -(grad_own + back)
    return (energy.reshape(blocks * atoms), forces.transpose(1, 0, 2).reshape(3, blocks * atoms))


def solution(mesh):
    placed = (
        P(None, ("gx", "gy")),
        P(("gx", "gy")),
        P(("gx", "gy"), None),
        P(("gx", "gy"), None, None, None),
        P("gx", "gy", None, None),
        P(),
        P(),
        P(),
        P(),
    )
    return jax.shard_map(
        local,
        mesh=mesh,
        in_specs=placed,
        out_specs=(P(("gx", "gy")), P(None, ("gx", "gy"))),
        check_vma=False,
    )
```

```python
import math

import jax
import jax.numpy as jnp
from jax import lax
from jax.sharding import PartitionSpec as P

OFFSETS = ((-1, -1), (-1, 0), (-1, 1), (0, -1), (0, 1), (1, -1), (1, 0), (1, 1))
HIGHEST = lax.Precision.HIGHEST


def harmonics(rel, dist):
    ux = rel[0] / dist
    uy = rel[1] / dist
    uz = rel[2] / dist
    root = math.sqrt(3.0)
    return jnp.stack(
        [
            jnp.ones_like(ux),
            ux,
            uy,
            uz,
            root * ux * uy,
            root * uy * uz,
            root * ux * uz,
            0.5 * root * (ux * ux - uy * uy),
            0.5 * (3.0 * uz * uz - 1.0),
        ]
    )


def tile_terms(own_pos, other_pos, other_feat, pair_mask, listed, count):
    atoms = own_pos.shape[1]
    centres = 0.5 + jnp.arange(count).astype(jnp.float32)
    rel = other_pos[:, None, :] - own_pos[:, :, None]
    dist = jnp.sqrt(jnp.sum(rel * rel, axis=0) + 0.25)
    offset = dist[None] - centres[:, None, None]
    basis = jnp.exp(-0.5 * offset * offset)
    angular = harmonics(rel, dist)
    weight = pair_mask.astype(jnp.float32) * (1.0 / math.sqrt(listed * atoms))
    tiles = (basis[:, None] * angular[None] * weight[None, None]).reshape(count * 9, atoms, atoms)
    return jnp.einsum(
        "qij,cj->qic", tiles.astype(jnp.bfloat16), other_feat, preferred_element_type=jnp.float32
    )


def atom_energy(own_pos, others_pos, others_feat, masks, radial, readin, readout):
    count = radial.shape[0]
    width = others_feat.shape[1]
    atoms = own_pos.shape[1]
    listed = others_pos.shape[0]
    total = jnp.zeros((count * 9, atoms, width), jnp.float32)
    for slot in range(listed):
        total = total + tile_terms(
            own_pos, others_pos[slot], others_feat[slot], masks[slot], listed, count
        )
    proj = total.reshape(count, 9, atoms, width)
    message = jnp.sum(radial[:, None, None, :] * proj, axis=0)
    first = jnp.sum(message[1:4] * message[1:4], axis=0)
    second = jnp.sum(message[4:9] * message[4:9], axis=0)
    invariants = jnp.concatenate([message[0], first, second], axis=1)
    hidden = jax.nn.silu(jnp.dot(invariants, readin, precision=HIGHEST))
    return jnp.dot(hidden, readout, precision=HIGHEST)


def select_slots(table, chosen):
    slots = table.shape[0]
    hit = chosen[..., None] == jnp.arange(slots, dtype=chosen.dtype)
    hit = hit.reshape(hit.shape + (1,) * (table.ndim - 1))
    return jnp.sum(jnp.where(hit, table, jnp.zeros((), table.dtype)), axis=2)


def halo(grid):
    count_x = lax.axis_size("gx")
    count_y = lax.axis_size("gy")
    up_x = [(i, (i + 1) % count_x) for i in range(count_x)]
    down_x = [((i + 1) % count_x, i) for i in range(count_x)]
    up_y = [(i, (i + 1) % count_y) for i in range(count_y)]
    down_y = [((i + 1) % count_y, i) for i in range(count_y)]
    from_left_y = lax.ppermute(grid[:, 2], "gy", up_y)
    from_right_y = lax.ppermute(grid[:, 0], "gy", down_y)
    columns = jnp.stack([from_left_y, grid[:, 1], from_right_y], axis=1)
    from_left_x = lax.ppermute(columns[2], "gx", up_x)
    from_right_x = lax.ppermute(columns[0], "gx", down_x)
    return jnp.stack([from_left_x, columns[1], from_right_x], axis=0)


def place(parts):
    empty = jnp.zeros_like(parts[0:1])
    full = jnp.concatenate([parts[:4], empty, parts[4:]], axis=0)
    return full.reshape((3, 3) + parts.shape[1:])


def collect(grid):
    return jnp.stack([grid[1 + pair[0], 1 + pair[1]] for pair in OFFSETS], axis=0)


def local(
    positions, species, neighbours, pair_masks, send_lists, embedding, radial, readin, readout
):
    atoms = pair_masks.shape[2]
    blocks = positions.shape[1] // atoms
    kinds = embedding.shape[0]
    sends = send_lists.shape[3]
    own_pos = positions.reshape(3, blocks, atoms).transpose(1, 0, 2)
    own_kind = species.reshape(blocks, 1, atoms).astype(jnp.float32)
    payload = jnp.concatenate([own_pos, own_kind], axis=1)
    chosen = send_lists.reshape(8, sends)
    pick = (chosen[:, :, None] == jnp.arange(blocks)).astype(jnp.float32)
    outgoing = jnp.einsum("dgb,bra->dgra", pick, payload, precision=HIGHEST)
    incoming = collect(halo(place(outgoing))).reshape(8 * sends, 4, atoms)
    ghost_pos = incoming[:, :3]
    ghost_kind = incoming[:, 3]

    def features(kind):
        onehot = (kind[None, :] == jnp.arange(kinds).astype(kind.dtype)[:, None]).astype(jnp.float32)
        return jnp.dot(embedding.T, onehot, precision=HIGHEST)

    own_feats32 = features(species).reshape(-1, blocks, atoms).transpose(1, 0, 2)
    ghost_feats32 = (
        features(ghost_kind.reshape(-1)).reshape(-1, 8 * sends, atoms).transpose(1, 0, 2)
    )

    def energies_of(own_now, ghost_now):
        table_pos = jnp.concatenate([own_now, ghost_now], axis=0)
        table_feat = jnp.concatenate([own_feats32, ghost_feats32], axis=0)
        others_pos = select_slots(table_pos, neighbours)
        others_feat = select_slots(table_feat, neighbours).astype(jnp.bfloat16)
        return jnp.stack(
            [
                atom_energy(
                    own_now[block],
                    others_pos[block],
                    others_feat[block],
                    pair_masks[block],
                    radial,
                    readin,
                    readout,
                )
                for block in range(blocks)
            ]
        )

    energy, pullback = jax.vjp(energies_of, own_pos, ghost_pos)
    grad_own, grad_ghost = pullback(jnp.ones_like(energy))
    returned = collect(halo(place(grad_ghost.reshape(8, sends, 3, atoms))))
    back = jnp.einsum("dgb,dgca->bca", pick, returned, precision=HIGHEST)
    forces = -(grad_own + back)
    return (energy.reshape(blocks * atoms), forces.transpose(1, 0, 2).reshape(3, blocks * atoms))


def solution(mesh):
    placed = (
        P(None, ("gx", "gy")),
        P(("gx", "gy")),
        P(("gx", "gy"), None),
        P(("gx", "gy"), None, None, None),
        P("gx", "gy", None, None),
        P(),
        P(),
        P(),
        P(),
    )
    return jax.shard_map(
        local,
        mesh=mesh,
        in_specs=placed,
        out_specs=(P(("gx", "gy")), P(None, ("gx", "gy"))),
        check_vma=False,
    )
```

```python
import math
from functools import partial

import jax
import jax.numpy as jnp
from jax import lax
from jax.experimental import pallas as pl
from jax.sharding import PartitionSpec as P

OFFSETS = ((-1, -1), (-1, 0), (-1, 1), (0, -1), (0, 1), (1, -1), (1, 0), (1, 1))
HIGHEST = lax.Precision.HIGHEST


def harmonics(rel, dist):
    ux = rel[0] / dist
    uy = rel[1] / dist
    uz = rel[2] / dist
    root = math.sqrt(3.0)
    return jnp.stack(
        [
            jnp.ones_like(ux),
            ux,
            uy,
            uz,
            root * ux * uy,
            root * uy * uz,
            root * ux * uz,
            0.5 * root * (ux * ux - uy * uy),
            0.5 * (3.0 * uz * uz - 1.0),
        ]
    )


def pair_kernel(own_ref, other_ref, weight_ref, feat_ref, out_ref):
    slot = pl.program_id(1)
    count = out_ref.shape[1] // 9
    rel = [other_ref[0, 0, d : d + 1, :] - own_ref[0, :, d : d + 1] for d in range(3)]
    dist = jnp.sqrt((rel[0] * rel[0] + rel[1] * rel[1] + rel[2] * rel[2]) + 0.25)
    angular = harmonics(rel, dist)
    weight = weight_ref[0, 0]
    feat = feat_ref[0, 0]
    for k in range(count):
        offset = dist - (0.5 + k)
        basis = jnp.exp(-0.5 * offset * offset)
        for m in range(9):
            tile = ((basis * angular[m]) * weight).astype(jnp.bfloat16)
            part = lax.dot_general(
                feat, tile, (((1,), (1,)), ((), ())), preferred_element_type=jnp.float32
            )
            q = k * 9 + m

            @pl.when(slot == 0)
            def _():
                out_ref[0, q] = part

            @pl.when(slot > 0)
            def _():
                out_ref[0, q] = out_ref[0, q] + part


def fused_proj(own_pos, others_pos, others_feat, weights, count):
    blocks, atoms = own_pos.shape[0], own_pos.shape[2]
    listed, width = others_pos.shape[1], others_feat.shape[2]
    return pl.pallas_call(
        pair_kernel,
        grid=(blocks, listed),
        in_specs=[
            pl.BlockSpec((1, atoms, 3), lambda b, n: (b, 0, 0)),
            pl.BlockSpec((1, 1, 3, atoms), lambda b, n: (b, n, 0, 0)),
            pl.BlockSpec((1, 1, atoms, atoms), lambda b, n: (b, n, 0, 0)),
            pl.BlockSpec((1, 1, width, atoms), lambda b, n: (b, n, 0, 0)),
        ],
        out_specs=pl.BlockSpec((1, count * 9, width, atoms), lambda b, n: (b, 0, 0, 0)),
        out_shape=jax.ShapeDtypeStruct((blocks, count * 9, width, atoms), jnp.float32),
    )(jnp.swapaxes(own_pos, 1, 2), others_pos, weights, others_feat)


def plain_proj(own_pos, others_pos, others_feat, weights, count):
    centres = 0.5 + jnp.arange(count).astype(jnp.float32)
    atoms = own_pos.shape[2]
    result = []
    for block in range(own_pos.shape[0]):
        total = 0.0
        for slot in range(others_pos.shape[1]):
            rel = others_pos[block, slot][:, None, :] - own_pos[block][:, :, None]
            dist = jnp.sqrt(jnp.sum(rel * rel, axis=0) + 0.25)
            offset = dist[None] - centres[:, None, None]
            basis = jnp.exp(-0.5 * offset * offset)
            angular = harmonics(rel, dist)
            tiles = basis[:, None] * angular[None] * weights[block, slot][None, None]
            tiles = tiles.reshape(count * 9, atoms, atoms).astype(jnp.bfloat16)
            total = total + jnp.einsum(
                "qij,cj->qci", tiles, others_feat[block, slot], preferred_element_type=jnp.float32
            )
        result.append(total)
    return jnp.stack(result)


@partial(jax.custom_vjp, nondiff_argnums=(4,))
def pair_proj(own_pos, others_pos, others_feat, weights, count):
    return fused_proj(own_pos, others_pos, others_feat, weights, count)


def pair_proj_fwd(own_pos, others_pos, others_feat, weights, count):
    return pair_proj(own_pos, others_pos, others_feat, weights, count), (
        own_pos,
        others_pos,
        others_feat,
        weights,
    )


def pair_proj_bwd(count, saved, grad):
    own_pos, others_pos, others_feat, weights = saved
    _, pullback = jax.vjp(
        lambda a, b: plain_proj(a, b, others_feat, weights, count), own_pos, others_pos
    )
    grad_own, grad_others = pullback(grad)
    return grad_own, grad_others, jnp.zeros_like(others_feat), jnp.zeros_like(weights)


pair_proj.defvjp(pair_proj_fwd, pair_proj_bwd)


def block_energies(proj, radial, readin, readout):
    count = radial.shape[0]
    proj = proj.reshape((proj.shape[0], count, 9) + proj.shape[2:])
    message = jnp.sum(radial[None, :, None, :, None] * proj, axis=1)
    first = jnp.sum(message[:, 1:4] * message[:, 1:4], axis=1)
    second = jnp.sum(message[:, 4:9] * message[:, 4:9], axis=1)
    invariants = jnp.concatenate([message[:, 0], first, second], axis=1)
    hidden = jax.nn.silu(jnp.einsum("fh,bfi->bhi", readin, invariants, precision=HIGHEST))
    return jnp.einsum("h,bhi->bi", readout, hidden, precision=HIGHEST)


def select_slots(table, chosen):
    slots = table.shape[0]
    hit = chosen[..., None] == jnp.arange(slots, dtype=chosen.dtype)
    hit = hit.reshape(hit.shape + (1,) * (table.ndim - 1))
    return jnp.sum(jnp.where(hit, table, jnp.zeros((), table.dtype)), axis=2)


def halo(grid):
    count_x = lax.axis_size("gx")
    count_y = lax.axis_size("gy")
    up_x = [(i, (i + 1) % count_x) for i in range(count_x)]
    down_x = [((i + 1) % count_x, i) for i in range(count_x)]
    up_y = [(i, (i + 1) % count_y) for i in range(count_y)]
    down_y = [((i + 1) % count_y, i) for i in range(count_y)]
    from_left_x = lax.ppermute(grid[2], "gx", up_x)
    from_right_x = lax.ppermute(grid[0], "gx", down_x)
    rows = jnp.stack([from_left_x, grid[1], from_right_x], axis=0)
    from_left_y = lax.ppermute(rows[:, 2], "gy", up_y)
    from_right_y = lax.ppermute(rows[:, 0], "gy", down_y)
    return jnp.stack([from_left_y, rows[:, 1], from_right_y], axis=1)


def place(parts):
    empty = jnp.zeros_like(parts[0:1])
    full = jnp.concatenate([parts[:4], empty, parts[4:]], axis=0)
    return full.reshape((3, 3) + parts.shape[1:])


def collect(grid):
    return jnp.stack([grid[1 + pair[0], 1 + pair[1]] for pair in OFFSETS], axis=0)


def local(
    positions, species, neighbours, pair_masks, send_lists, embedding, radial, readin, readout
):
    atoms = pair_masks.shape[2]
    blocks = positions.shape[1] // atoms
    kinds = embedding.shape[0]
    sends = send_lists.shape[3]
    own_pos = positions.reshape(3, blocks, atoms).transpose(1, 0, 2)
    own_kind = species.reshape(blocks, 1, atoms).astype(jnp.float32)
    payload = jnp.concatenate([own_pos, own_kind], axis=1)
    chosen = send_lists.reshape(8, sends)
    pick = (chosen[:, :, None] == jnp.arange(blocks)).astype(jnp.float32)
    outgoing = jnp.einsum("dgb,bra->dgra", pick, payload, precision=HIGHEST)
    incoming = collect(halo(place(outgoing))).reshape(8 * sends, 4, atoms)
    ghost_pos = incoming[:, :3]
    ghost_kind = incoming[:, 3]

    def features(kind):
        onehot = (kind[None, :] == jnp.arange(kinds).astype(kind.dtype)[:, None]).astype(jnp.float32)
        return jnp.dot(embedding.T, onehot, precision=HIGHEST)

    own_feats32 = features(species).reshape(-1, blocks, atoms).transpose(1, 0, 2)
    ghost_feats32 = (
        features(ghost_kind.reshape(-1)).reshape(-1, 8 * sends, atoms).transpose(1, 0, 2)
    )

    listed = neighbours.shape[1]
    weights = pair_masks.astype(jnp.float32) * (1.0 / math.sqrt(listed * atoms))

    def energies_of(own_now, ghost_now):
        table_pos = jnp.concatenate([own_now, ghost_now], axis=0)
        table_feat = jnp.concatenate([own_feats32, ghost_feats32], axis=0)
        others_pos = select_slots(table_pos, neighbours)
        others_feat = select_slots(table_feat, neighbours).astype(jnp.bfloat16)
        proj = pair_proj(own_now, others_pos, others_feat, weights, radial.shape[0])
        return block_energies(proj, radial, readin, readout)

    energy, pullback = jax.vjp(energies_of, own_pos, ghost_pos)
    grad_own, grad_ghost = pullback(jnp.ones_like(energy))
    returned = collect(halo(place(grad_ghost.reshape(8, sends, 3, atoms))))
    back = jnp.einsum("dgb,dgca->bca", pick, returned, precision=HIGHEST)
    forces = -(grad_own + back)
    return (energy.reshape(blocks * atoms), forces.transpose(1, 0, 2).reshape(3, blocks * atoms))


def solution(mesh):
    placed = (
        P(None, ("gx", "gy")),
        P(("gx", "gy")),
        P(("gx", "gy"), None),
        P(("gx", "gy"), None, None, None),
        P("gx", "gy", None, None),
        P(),
        P(),
        P(),
        P(),
    )
    return jax.shard_map(
        local,
        mesh=mesh,
        in_specs=placed,
        out_specs=(P(("gx", "gy")), P(None, ("gx", "gy"))),
        check_vma=False,
    )
```

```python
import math
from functools import partial

import jax
import jax.numpy as jnp
from jax import lax
from jax.experimental import pallas as pl
from jax.sharding import PartitionSpec as P

OFFSETS = ((-1, -1), (-1, 0), (-1, 1), (0, -1), (0, 1), (1, -1), (1, 0), (1, 1))
HIGHEST = lax.Precision.HIGHEST


def harmonics(rel, dist):
    ux = rel[0] / dist
    uy = rel[1] / dist
    uz = rel[2] / dist
    root = math.sqrt(3.0)
    return jnp.stack(
        [
            jnp.ones_like(ux),
            ux,
            uy,
            uz,
            root * ux * uy,
            root * uy * uz,
            root * ux * uz,
            0.5 * root * (ux * ux - uy * uy),
            0.5 * (3.0 * uz * uz - 1.0),
        ]
    )


def pair_kernel(own_ref, other_ref, weight_ref, feat_ref, out_ref):
    count = out_ref.shape[1] // 9
    for slot in range(other_ref.shape[1]):
        rel = [other_ref[0, slot, d : d + 1, :] - own_ref[0, :, d : d + 1] for d in range(3)]
        dist = jnp.sqrt((rel[0] * rel[0] + rel[1] * rel[1] + rel[2] * rel[2]) + 0.25)
        angular = harmonics(rel, dist)
        weight = weight_ref[0, slot]
        feat = feat_ref[0, slot]
        for k in range(count):
            offset = dist - (0.5 + k)
            basis = jnp.exp(-0.5 * offset * offset)
            for m in range(9):
                tile = ((basis * angular[m]) * weight).astype(jnp.bfloat16)
                part = jnp.dot(tile, feat, preferred_element_type=jnp.float32)
                if slot == 0:
                    out_ref[0, k * 9 + m] = part
                else:
                    out_ref[0, k * 9 + m] = out_ref[0, k * 9 + m] + part


def fused_proj(own_pos, others_pos, others_feat, weights, count):
    blocks, atoms = own_pos.shape[0], own_pos.shape[2]
    listed, width = others_pos.shape[1], others_feat.shape[2]
    return pl.pallas_call(
        pair_kernel,
        grid=(blocks,),
        in_specs=[
            pl.BlockSpec((1, atoms, 3), lambda b: (b, 0, 0)),
            pl.BlockSpec((1, listed, 3, atoms), lambda b: (b, 0, 0, 0)),
            pl.BlockSpec((1, listed, atoms, atoms), lambda b: (b, 0, 0, 0)),
            pl.BlockSpec((1, listed, atoms, width), lambda b: (b, 0, 0, 0)),
        ],
        out_specs=pl.BlockSpec((1, count * 9, atoms, width), lambda b: (b, 0, 0, 0)),
        out_shape=jax.ShapeDtypeStruct((blocks, count * 9, atoms, width), jnp.float32),
    )(jnp.swapaxes(own_pos, 1, 2), others_pos, weights, jnp.swapaxes(others_feat, 2, 3))


def plain_proj(own_pos, others_pos, others_feat, weights, count):
    centres = 0.5 + jnp.arange(count).astype(jnp.float32)
    atoms = own_pos.shape[2]
    result = []
    for block in range(own_pos.shape[0]):
        total = 0.0
        for slot in range(others_pos.shape[1]):
            rel = others_pos[block, slot][:, None, :] - own_pos[block][:, :, None]
            dist = jnp.sqrt(jnp.sum(rel * rel, axis=0) + 0.25)
            offset = dist[None] - centres[:, None, None]
            basis = jnp.exp(-0.5 * offset * offset)
            angular = harmonics(rel, dist)
            tiles = basis[:, None] * angular[None] * weights[block, slot][None, None]
            tiles = tiles.reshape(count * 9, atoms, atoms).astype(jnp.bfloat16)
            total = total + jnp.einsum(
                "qij,cj->qic", tiles, others_feat[block, slot], preferred_element_type=jnp.float32
            )
        result.append(total)
    return jnp.stack(result)


@partial(jax.custom_vjp, nondiff_argnums=(4,))
def pair_proj(own_pos, others_pos, others_feat, weights, count):
    return fused_proj(own_pos, others_pos, others_feat, weights, count)


def pair_proj_fwd(own_pos, others_pos, others_feat, weights, count):
    return pair_proj(own_pos, others_pos, others_feat, weights, count), (
        own_pos,
        others_pos,
        others_feat,
        weights,
    )


def pair_proj_bwd(count, saved, grad):
    own_pos, others_pos, others_feat, weights = saved
    _, pullback = jax.vjp(
        lambda a, b: plain_proj(a, b, others_feat, weights, count), own_pos, others_pos
    )
    grad_own, grad_others = pullback(grad)
    return grad_own, grad_others, jnp.zeros_like(others_feat), jnp.zeros_like(weights)


pair_proj.defvjp(pair_proj_fwd, pair_proj_bwd)


def block_energies(proj, radial, readin, readout):
    count = radial.shape[0]
    proj = proj.reshape((proj.shape[0], count, 9) + proj.shape[2:])
    message = jnp.sum(radial[None, :, None, None, :] * proj, axis=1)
    first = jnp.sum(message[:, 1:4] * message[:, 1:4], axis=1)
    second = jnp.sum(message[:, 4:9] * message[:, 4:9], axis=1)
    invariants = jnp.concatenate([message[:, 0], first, second], axis=2)
    hidden = jax.nn.silu(jnp.einsum("bif,fh->bih", invariants, readin, precision=HIGHEST))
    return jnp.einsum("bih,h->bi", hidden, readout, precision=HIGHEST)


def select_slots(table, chosen):
    slots = table.shape[0]
    hit = chosen[..., None] == jnp.arange(slots, dtype=chosen.dtype)
    hit = hit.reshape(hit.shape + (1,) * (table.ndim - 1))
    return jnp.sum(jnp.where(hit, table, jnp.zeros((), table.dtype)), axis=2)


def halo(grid):
    count_x = lax.axis_size("gx")
    count_y = lax.axis_size("gy")
    up_x = [(i, (i + 1) % count_x) for i in range(count_x)]
    down_x = [((i + 1) % count_x, i) for i in range(count_x)]
    up_y = [(i, (i + 1) % count_y) for i in range(count_y)]
    down_y = [((i + 1) % count_y, i) for i in range(count_y)]
    from_left_x = lax.ppermute(grid[2], "gx", up_x)
    from_right_x = lax.ppermute(grid[0], "gx", down_x)
    rows = jnp.stack([from_left_x, grid[1], from_right_x], axis=0)
    from_left_y = lax.ppermute(rows[:, 2], "gy", up_y)
    from_right_y = lax.ppermute(rows[:, 0], "gy", down_y)
    return jnp.stack([from_left_y, rows[:, 1], from_right_y], axis=1)


def place(parts):
    empty = jnp.zeros_like(parts[0:1])
    full = jnp.concatenate([parts[:4], empty, parts[4:]], axis=0)
    return full.reshape((3, 3) + parts.shape[1:])


def collect(grid):
    return jnp.stack([grid[1 + pair[0], 1 + pair[1]] for pair in OFFSETS], axis=0)


def local(
    positions, species, neighbours, pair_masks, send_lists, embedding, radial, readin, readout
):
    atoms = pair_masks.shape[2]
    blocks = positions.shape[1] // atoms
    kinds = embedding.shape[0]
    sends = send_lists.shape[3]
    own_pos = positions.reshape(3, blocks, atoms).transpose(1, 0, 2)
    own_kind = species.reshape(blocks, 1, atoms).astype(jnp.float32)
    payload = jnp.concatenate([own_pos, own_kind], axis=1)
    chosen = send_lists.reshape(8, sends)
    pick = (chosen[:, :, None] == jnp.arange(blocks)).astype(jnp.float32)
    outgoing = jnp.einsum("dgb,bra->dgra", pick, payload, precision=HIGHEST)
    incoming = collect(halo(place(outgoing))).reshape(8 * sends, 4, atoms)
    ghost_pos = incoming[:, :3]
    ghost_kind = incoming[:, 3]

    def features(kind):
        onehot = (kind[None, :] == jnp.arange(kinds).astype(kind.dtype)[:, None]).astype(jnp.float32)
        return jnp.dot(embedding.T, onehot, precision=HIGHEST)

    own_feats32 = features(species).reshape(-1, blocks, atoms).transpose(1, 0, 2)
    ghost_feats32 = (
        features(ghost_kind.reshape(-1)).reshape(-1, 8 * sends, atoms).transpose(1, 0, 2)
    )

    listed = neighbours.shape[1]
    weights = pair_masks.astype(jnp.float32) * (1.0 / math.sqrt(listed * atoms))

    def energies_of(own_now, ghost_now):
        table_pos = jnp.concatenate([own_now, ghost_now], axis=0)
        table_feat = jnp.concatenate([own_feats32, ghost_feats32], axis=0)
        others_pos = select_slots(table_pos, neighbours)
        others_feat = select_slots(table_feat, neighbours).astype(jnp.bfloat16)
        proj = pair_proj(own_now, others_pos, others_feat, weights, radial.shape[0])
        return block_energies(proj, radial, readin, readout)

    energy, pullback = jax.vjp(energies_of, own_pos, ghost_pos)
    grad_own, grad_ghost = pullback(jnp.ones_like(energy))
    returned = collect(halo(place(grad_ghost.reshape(8, sends, 3, atoms))))
    back = jnp.einsum("dgb,dgca->bca", pick, returned, precision=HIGHEST)
    forces = -(grad_own + back)
    return (energy.reshape(blocks * atoms), forces.transpose(1, 0, 2).reshape(3, blocks * atoms))


def solution(mesh):
    placed = (
        P(None, ("gx", "gy")),
        P(("gx", "gy")),
        P(("gx", "gy"), None),
        P(("gx", "gy"), None, None, None),
        P("gx", "gy", None, None),
        P(),
        P(),
        P(),
        P(),
    )
    return jax.shard_map(
        local,
        mesh=mesh,
        in_specs=placed,
        out_specs=(P(("gx", "gy")), P(None, ("gx", "gy"))),
        check_vma=False,
    )
```

```python
import math

import jax
import jax.numpy as jnp
from jax import lax
from jax.sharding import PartitionSpec as P

OFFSETS = ((-1, -1), (-1, 0), (-1, 1), (0, -1), (0, 1), (1, -1), (1, 0), (1, 1))
HIGHEST = lax.Precision.HIGHEST


def harmonics(rel, dist):
    ux = rel[0] / dist
    uy = rel[1] / dist
    uz = rel[2] / dist
    root = math.sqrt(3.0)
    return jnp.stack(
        [
            jnp.ones_like(ux),
            ux,
            uy,
            uz,
            root * ux * uy,
            root * uy * uz,
            root * ux * uz,
            0.5 * root * (ux * ux - uy * uy),
            0.5 * (3.0 * uz * uz - 1.0),
        ]
    )


def tile_terms(own_pos, other_pos, other_feat, pair_mask, listed, count):
    atoms = own_pos.shape[1]
    centres = 0.5 + jnp.arange(count).astype(jnp.float32)
    rel = other_pos[:, None, :] - own_pos[:, :, None]
    dist = jnp.sqrt(jnp.sum(rel * rel, axis=0) + 0.25)
    offset = dist[None] - centres[:, None, None]
    basis = jnp.exp(-0.5 * offset * offset)
    angular = harmonics(rel, dist)
    weight = pair_mask.astype(jnp.float32) * (1.0 / math.sqrt(listed * atoms))
    tiles = (basis[:, None] * angular[None] * weight[None, None]).reshape(count * 9, atoms, atoms)
    return jnp.einsum(
        "qij,cj->qci", tiles.astype(jnp.bfloat16), other_feat, preferred_element_type=jnp.float32
    )


def atom_energy(own_pos, others_pos, others_feat, masks, radial, readin, readout):
    count = radial.shape[0]
    width = others_feat.shape[1]
    atoms = own_pos.shape[1]
    listed = others_pos.shape[0]
    total = jnp.zeros((count * 9, width, atoms), jnp.float32)
    for slot in range(listed):
        total = total + tile_terms(
            own_pos, others_pos[slot], others_feat[slot], masks[slot], listed, count
        )
    proj = total.reshape(count, 9, width, atoms)
    message = jnp.sum(radial[:, None, :, None] * proj, axis=0)
    first = jnp.sum(message[1:4] * message[1:4], axis=0)
    second = jnp.sum(message[4:9] * message[4:9], axis=0)
    invariants = jnp.concatenate([message[0], first, second], axis=0)
    hidden = jax.nn.silu(jnp.dot(readin.T, invariants, precision=HIGHEST))
    return jnp.dot(readout, hidden, precision=HIGHEST)


def select_slots(table, chosen):
    slots = table.shape[0]
    hit = chosen[..., None] == jnp.arange(slots, dtype=chosen.dtype)
    hit = hit.reshape(hit.shape + (1,) * (table.ndim - 1))
    return jnp.sum(jnp.where(hit, table, jnp.zeros((), table.dtype)), axis=2)


def halo(grid):
    count_x = lax.axis_size("gx")
    count_y = lax.axis_size("gy")
    up_x = [(i, (i + 1) % count_x) for i in range(count_x)]
    down_x = [((i + 1) % count_x, i) for i in range(count_x)]
    up_y = [(i, (i + 1) % count_y) for i in range(count_y)]
    down_y = [((i + 1) % count_y, i) for i in range(count_y)]
    from_left_x = lax.ppermute(grid[2], "gx", up_x)
    from_right_x = lax.ppermute(grid[0], "gx", down_x)
    rows = jnp.stack([from_left_x, grid[1], from_right_x], axis=0)
    from_left_y = lax.ppermute(rows[:, 2], "gy", up_y)
    from_right_y = lax.ppermute(rows[:, 0], "gy", down_y)
    return jnp.stack([from_left_y, rows[:, 1], from_right_y], axis=1)


def place(parts):
    empty = jnp.zeros_like(parts[0:1])
    full = jnp.concatenate([parts[:4], empty, parts[4:]], axis=0)
    return full.reshape((3, 3) + parts.shape[1:])


def collect(grid):
    return jnp.stack([grid[1 + pair[0], 1 + pair[1]] for pair in OFFSETS], axis=0)


def local(
    positions, species, neighbours, pair_masks, send_lists, embedding, radial, readin, readout
):
    atoms = pair_masks.shape[2]
    blocks = positions.shape[1] // atoms
    kinds = embedding.shape[0]
    sends = send_lists.shape[3]
    own_pos = positions.reshape(3, blocks, atoms).transpose(1, 0, 2)
    own_kind = species.reshape(blocks, 1, atoms).astype(jnp.float32)
    payload = jnp.concatenate([own_pos, own_kind], axis=1)
    chosen = send_lists.reshape(8, sends)
    pick = (chosen[:, :, None] == jnp.arange(blocks)).astype(jnp.float32)
    outgoing = jnp.einsum("dgb,bra->dgra", pick, payload, precision=HIGHEST)
    incoming = collect(halo(place(outgoing))).reshape(8 * sends, 4, atoms)
    ghost_pos = incoming[:, :3]
    ghost_kind = incoming[:, 3]

    def features(kind):
        hit = kind[None, None, :] == jnp.arange(kinds).astype(kind.dtype)[:, None, None]
        return jnp.sum(jnp.where(hit, embedding[:, :, None], 0.0), axis=0)

    own_feats32 = features(species).reshape(-1, blocks, atoms).transpose(1, 0, 2)
    ghost_feats32 = (
        features(ghost_kind.reshape(-1)).reshape(-1, 8 * sends, atoms).transpose(1, 0, 2)
    )

    def energies_of(own_now, ghost_now):
        table_pos = jnp.concatenate([own_now, ghost_now], axis=0)
        table_feat = jnp.concatenate([own_feats32, ghost_feats32], axis=0)
        others_pos = select_slots(table_pos, neighbours)
        others_feat = select_slots(table_feat, neighbours).astype(jnp.bfloat16)
        return jnp.stack(
            [
                atom_energy(
                    own_now[block],
                    others_pos[block],
                    others_feat[block],
                    pair_masks[block],
                    radial,
                    readin,
                    readout,
                )
                for block in range(blocks)
            ]
        )

    energy, pullback = jax.vjp(energies_of, own_pos, ghost_pos)
    grad_own, grad_ghost = pullback(jnp.ones_like(energy))
    returned = collect(halo(place(grad_ghost.reshape(8, sends, 3, atoms))))
    back = jnp.sum(
        jnp.where(pick[:, :, :, None, None] > 0, returned[:, :, None], 0.0), axis=(0, 1)
    )
    forces = -(grad_own + back)
    return (energy.reshape(blocks * atoms), forces.transpose(1, 0, 2).reshape(3, blocks * atoms))


def solution(mesh):
    placed = (
        P(None, ("gx", "gy")),
        P(("gx", "gy")),
        P(("gx", "gy"), None),
        P(("gx", "gy"), None, None, None),
        P("gx", "gy", None, None),
        P(),
        P(),
        P(),
        P(),
    )
    return jax.shard_map(
        local,
        mesh=mesh,
        in_specs=placed,
        out_specs=(P(("gx", "gy")), P(None, ("gx", "gy"))),
        check_vma=False,
    )
```

```python
import math

import jax
import jax.numpy as jnp
from jax import lax
from jax.sharding import PartitionSpec as P

OFFSETS = ((-1, -1), (-1, 0), (-1, 1), (0, -1), (0, 1), (1, -1), (1, 0), (1, 1))
HIGHEST = lax.Precision.HIGHEST


def harmonics(rel, dist):
    ux = rel[0] / dist
    uy = rel[1] / dist
    uz = rel[2] / dist
    root = math.sqrt(3.0)
    return jnp.stack(
        [
            jnp.ones_like(ux),
            ux,
            uy,
            uz,
            root * ux * uy,
            root * uy * uz,
            root * ux * uz,
            0.5 * root * (ux * ux - uy * uy),
            0.5 * (3.0 * uz * uz - 1.0),
        ]
    )


def tile_terms(own_pos, other_pos, other_feat, pair_mask, listed, count):
    atoms = own_pos.shape[1]
    centres = 0.5 + jnp.arange(count).astype(jnp.float32)
    rel = other_pos[:, None, :] - own_pos[:, :, None]
    dist = jnp.sqrt(jnp.sum(rel * rel, axis=0) + 0.25)
    offset = dist[None] - centres[:, None, None]
    basis = jnp.exp(-0.5 * offset * offset)
    angular = harmonics(rel, dist)
    weight = pair_mask.astype(jnp.float32) * (1.0 / math.sqrt(listed * atoms))
    tiles = (basis[:, None] * angular[None] * weight[None, None]).reshape(count * 9, atoms, atoms)
    return jnp.einsum(
        "qij,cj->qci", tiles.astype(jnp.bfloat16), other_feat, preferred_element_type=jnp.float32
    )


def atom_energy(own_pos, others_pos, others_feat, masks, radial, readin, readout):
    count = radial.shape[0]
    width = others_feat.shape[1]
    atoms = own_pos.shape[1]
    listed = others_pos.shape[0]
    total = jnp.zeros((count * 9, width, atoms), jnp.float32)
    for slot in range(listed):
        total = total + tile_terms(
            own_pos, others_pos[slot], others_feat[slot], masks[slot], listed, count
        )
    proj = total.reshape(count, 9, width, atoms)
    message = jnp.sum(radial[:, None, :, None] * proj, axis=0)
    first = jnp.sum(message[1:4] * message[1:4], axis=0)
    second = jnp.sum(message[4:9] * message[4:9], axis=0)
    invariants = jnp.concatenate([message[0], first, second], axis=0)
    hidden = jax.nn.silu(jnp.dot(readin.T, invariants, precision=HIGHEST))
    return jnp.dot(readout, hidden, precision=HIGHEST)


def select_slots(table, chosen):
    slots = table.shape[0]
    hit = chosen[..., None] == jnp.arange(slots, dtype=chosen.dtype)
    hit = hit.reshape(hit.shape + (1,) * (table.ndim - 1))
    return jnp.sum(jnp.where(hit, table, jnp.zeros((), table.dtype)), axis=2)


def neighbourhood(own):
    count_x = lax.axis_size("gx")
    count_y = lax.axis_size("gy")
    up_x = [(i, (i + 1) % count_x) for i in range(count_x)]
    down_x = [((i + 1) % count_x, i) for i in range(count_x)]
    up_y = [(i, (i + 1) % count_y) for i in range(count_y)]
    down_y = [((i + 1) % count_y, i) for i in range(count_y)]
    column = jnp.stack(
        [lax.ppermute(own, "gx", up_x), own, lax.ppermute(own, "gx", down_x)], axis=0
    )
    return jnp.stack(
        [lax.ppermute(column, "gy", up_y), column, lax.ppermute(column, "gy", down_y)], axis=1
    )


def halo(grid):
    count_x = lax.axis_size("gx")
    count_y = lax.axis_size("gy")
    up_x = [(i, (i + 1) % count_x) for i in range(count_x)]
    down_x = [((i + 1) % count_x, i) for i in range(count_x)]
    up_y = [(i, (i + 1) % count_y) for i in range(count_y)]
    down_y = [((i + 1) % count_y, i) for i in range(count_y)]
    from_left_x = lax.ppermute(grid[2], "gx", up_x)
    from_right_x = lax.ppermute(grid[0], "gx", down_x)
    rows = jnp.stack([from_left_x, grid[1], from_right_x], axis=0)
    from_left_y = lax.ppermute(rows[:, 2], "gy", up_y)
    from_right_y = lax.ppermute(rows[:, 0], "gy", down_y)
    return jnp.stack([from_left_y, rows[:, 1], from_right_y], axis=1)


def place(parts):
    empty = jnp.zeros_like(parts[0:1])
    full = jnp.concatenate([parts[:4], empty, parts[4:]], axis=0)
    return full.reshape((3, 3) + parts.shape[1:])


def collect(grid):
    return jnp.stack([grid[1 + pair[0], 1 + pair[1]] for pair in OFFSETS], axis=0)


def local(
    positions, species, neighbours, pair_masks, send_lists, embedding, radial, readin, readout
):
    atoms = pair_masks.shape[2]
    blocks = positions.shape[1] // atoms
    kinds = embedding.shape[0]
    sends = send_lists.shape[3]
    own_pos = positions.reshape(3, blocks, atoms).transpose(1, 0, 2)
    chosen = send_lists.reshape(8, sends)
    pick = (chosen[:, :, None] == jnp.arange(blocks)).astype(jnp.float32)
    raw = jnp.concatenate([positions, species.astype(jnp.float32)[None]], axis=0)
    raw = raw.reshape(4 * blocks, atoms)
    listing = jnp.zeros((atoms,), jnp.float32).at[: 8 * sends].set(
        chosen.astype(jnp.float32).reshape(-1)
    )
    payload = jnp.concatenate([raw, listing[None]], axis=0)
    near = neighbourhood(payload)
    incoming = []
    for d, pair in enumerate(OFFSETS):
        cell = near[1 + pair[0], 1 + pair[1]]
        rows = cell[: 4 * blocks].reshape(4, blocks, atoms)
        sent = cell[4 * blocks, : 8 * sends].reshape(8, sends)[7 - d]
        for g in range(sends):
            hit = sent[g] == jnp.arange(blocks).astype(jnp.float32)
            incoming.append(jnp.sum(jnp.where(hit[None, :, None], rows, 0.0), axis=1))
    incoming = jnp.stack(incoming)
    ghost_pos = incoming[:, :3]
    ghost_kind = incoming[:, 3]

    def features(kind):
        onehot = (kind[None, :] == jnp.arange(kinds).astype(kind.dtype)[:, None]).astype(jnp.float32)
        return jnp.dot(embedding.T, onehot, precision=HIGHEST)

    own_feats32 = features(species).reshape(-1, blocks, atoms).transpose(1, 0, 2)
    ghost_feats32 = (
        features(ghost_kind.reshape(-1)).reshape(-1, 8 * sends, atoms).transpose(1, 0, 2)
    )

    def energies_of(own_now, ghost_now):
        table_pos = jnp.concatenate([own_now, ghost_now], axis=0)
        table_feat = jnp.concatenate([own_feats32, ghost_feats32], axis=0)
        others_pos = select_slots(table_pos, neighbours)
        others_feat = select_slots(table_feat, neighbours).astype(jnp.bfloat16)
        return jnp.stack(
            [
                atom_energy(
                    own_now[block],
                    others_pos[block],
                    others_feat[block],
                    pair_masks[block],
                    radial,
                    readin,
                    readout,
                )
                for block in range(blocks)
            ]
        )

    energy, pullback = jax.vjp(energies_of, own_pos, ghost_pos)
    grad_own, grad_ghost = pullback(jnp.ones_like(energy))
    returned = collect(halo(place(grad_ghost.reshape(8, sends, 3, atoms))))
    back = jnp.einsum("dgb,dgca->bca", pick, returned, precision=HIGHEST)
    forces = -(grad_own + back)
    return (energy.reshape(blocks * atoms), forces.transpose(1, 0, 2).reshape(3, blocks * atoms))


def solution(mesh):
    placed = (
        P(None, ("gx", "gy")),
        P(("gx", "gy")),
        P(("gx", "gy"), None),
        P(("gx", "gy"), None, None, None),
        P("gx", "gy", None, None),
        P(),
        P(),
        P(),
        P(),
    )
    return jax.shard_map(
        local,
        mesh=mesh,
        in_specs=placed,
        out_specs=(P(("gx", "gy")), P(None, ("gx", "gy"))),
        check_vma=False,
    )
```

```python
import math

import jax
import jax.numpy as jnp
from jax import lax
from jax.sharding import PartitionSpec as P

OFFSETS = ((-1, -1), (-1, 0), (-1, 1), (0, -1), (0, 1), (1, -1), (1, 0), (1, 1))
HIGHEST = lax.Precision.HIGHEST


def harmonics(rel, dist):
    ux = rel[0] / dist
    uy = rel[1] / dist
    uz = rel[2] / dist
    root = math.sqrt(3.0)
    return jnp.stack(
        [
            jnp.ones_like(ux),
            ux,
            uy,
            uz,
            root * ux * uy,
            root * uy * uz,
            root * ux * uz,
            0.5 * root * (ux * ux - uy * uy),
            0.5 * (3.0 * uz * uz - 1.0),
        ]
    )


def tile_terms(own_pos, other_pos, other_feat, pair_mask, listed, count):
    atoms = own_pos.shape[1]
    centres = 0.5 + jnp.arange(count).astype(jnp.float32)
    rel = other_pos[:, None, :] - own_pos[:, :, None]
    dist = jnp.sqrt(jnp.sum(rel * rel, axis=0) + 0.25)
    offset = dist[None] - centres[:, None, None]
    basis = jnp.exp(-0.5 * offset * offset)
    angular = harmonics(rel, dist)
    weight = pair_mask.astype(jnp.float32) * (1.0 / math.sqrt(listed * atoms))
    tiles = (basis[:, None] * angular[None] * weight[None, None]).reshape(count * 9, atoms, atoms)
    return jnp.einsum(
        "qij,cj->qci", tiles.astype(jnp.bfloat16), other_feat, preferred_element_type=jnp.float32
    )


def atom_energy(own_pos, others_pos, others_feat, masks, radial, readin, readout):
    count = radial.shape[0]
    width = others_feat.shape[1]
    atoms = own_pos.shape[1]
    listed = others_pos.shape[0]
    total = jnp.zeros((count * 9, width, atoms), jnp.float32)
    for slot in range(listed):
        total = total + tile_terms(
            own_pos, others_pos[slot], others_feat[slot], masks[slot], listed, count
        )
    proj = total.reshape(count, 9, width, atoms)
    message = jnp.sum(radial[:, None, :, None] * proj, axis=0)
    first = jnp.sum(message[1:4] * message[1:4], axis=0)
    second = jnp.sum(message[4:9] * message[4:9], axis=0)
    invariants = jnp.concatenate([message[0], first, second], axis=0)
    hidden = jax.nn.silu(jnp.dot(readin.T, invariants, precision=lax.Precision.HIGH))
    return jnp.dot(readout, hidden, precision=lax.Precision.HIGH)


def select_slots(table, chosen):
    slots = table.shape[0]
    hit = chosen[..., None] == jnp.arange(slots, dtype=chosen.dtype)
    hit = hit.reshape(hit.shape + (1,) * (table.ndim - 1))
    return jnp.sum(jnp.where(hit, table, jnp.zeros((), table.dtype)), axis=2)


def halo(grid):
    count_x = lax.axis_size("gx")
    count_y = lax.axis_size("gy")
    up_x = [(i, (i + 1) % count_x) for i in range(count_x)]
    down_x = [((i + 1) % count_x, i) for i in range(count_x)]
    up_y = [(i, (i + 1) % count_y) for i in range(count_y)]
    down_y = [((i + 1) % count_y, i) for i in range(count_y)]
    from_left_x = lax.ppermute(grid[2], "gx", up_x)
    from_right_x = lax.ppermute(grid[0], "gx", down_x)
    rows = jnp.stack([from_left_x, grid[1], from_right_x], axis=0)
    from_left_y = lax.ppermute(rows[:, 2], "gy", up_y)
    from_right_y = lax.ppermute(rows[:, 0], "gy", down_y)
    return jnp.stack([from_left_y, rows[:, 1], from_right_y], axis=1)


def place(parts):
    empty = jnp.zeros_like(parts[0:1])
    full = jnp.concatenate([parts[:4], empty, parts[4:]], axis=0)
    return full.reshape((3, 3) + parts.shape[1:])


def collect(grid):
    return jnp.stack([grid[1 + pair[0], 1 + pair[1]] for pair in OFFSETS], axis=0)


def local(
    positions, species, neighbours, pair_masks, send_lists, embedding, radial, readin, readout
):
    atoms = pair_masks.shape[2]
    blocks = positions.shape[1] // atoms
    kinds = embedding.shape[0]
    sends = send_lists.shape[3]
    own_pos = positions.reshape(3, blocks, atoms).transpose(1, 0, 2)
    own_kind = species.reshape(blocks, 1, atoms).astype(jnp.float32)
    payload = jnp.concatenate([own_pos, own_kind], axis=1)
    chosen = send_lists.reshape(8, sends)
    pick = (chosen[:, :, None] == jnp.arange(blocks)).astype(jnp.float32)
    outgoing = jnp.einsum("dgb,bra->dgra", pick, payload, precision=HIGHEST)
    incoming = collect(halo(place(outgoing))).reshape(8 * sends, 4, atoms)
    ghost_pos = incoming[:, :3]
    ghost_kind = incoming[:, 3]

    def features(kind):
        onehot = (kind[None, :] == jnp.arange(kinds).astype(kind.dtype)[:, None]).astype(jnp.float32)
        return jnp.dot(embedding.T, onehot, precision=HIGHEST)

    own_feats32 = features(species).reshape(-1, blocks, atoms).transpose(1, 0, 2)
    ghost_feats32 = (
        features(ghost_kind.reshape(-1)).reshape(-1, 8 * sends, atoms).transpose(1, 0, 2)
    )

    def energies_of(own_now, ghost_now):
        table_pos = jnp.concatenate([own_now, ghost_now], axis=0)
        table_feat = jnp.concatenate([own_feats32, ghost_feats32], axis=0)
        others_pos = select_slots(table_pos, neighbours)
        others_feat = select_slots(table_feat, neighbours).astype(jnp.bfloat16)
        return jnp.stack(
            [
                atom_energy(
                    own_now[block],
                    others_pos[block],
                    others_feat[block],
                    pair_masks[block],
                    radial,
                    readin,
                    readout,
                )
                for block in range(blocks)
            ]
        )

    energy, pullback = jax.vjp(energies_of, own_pos, ghost_pos)
    grad_own, grad_ghost = pullback(jnp.ones_like(energy))
    returned = collect(halo(place(grad_ghost.reshape(8, sends, 3, atoms))))
    back = jnp.einsum("dgb,dgca->bca", pick, returned, precision=HIGHEST)
    forces = -(grad_own + back)
    return (energy.reshape(blocks * atoms), forces.transpose(1, 0, 2).reshape(3, blocks * atoms))


def solution(mesh):
    placed = (
        P(None, ("gx", "gy")),
        P(("gx", "gy")),
        P(("gx", "gy"), None),
        P(("gx", "gy"), None, None, None),
        P("gx", "gy", None, None),
        P(),
        P(),
        P(),
        P(),
    )
    return jax.shard_map(
        local,
        mesh=mesh,
        in_specs=placed,
        out_specs=(P(("gx", "gy")), P(None, ("gx", "gy"))),
        check_vma=False,
    )
```

```python
import math

import jax
import jax.numpy as jnp
from jax import lax
from jax.sharding import PartitionSpec as P

OFFSETS = ((-1, -1), (-1, 0), (-1, 1), (0, -1), (0, 1), (1, -1), (1, 0), (1, 1))
HIGHEST = lax.Precision.HIGHEST


def harmonics(rel, dist):
    ux = rel[0] / dist
    uy = rel[1] / dist
    uz = rel[2] / dist
    root = math.sqrt(3.0)
    return jnp.stack(
        [
            jnp.ones_like(ux),
            ux,
            uy,
            uz,
            root * ux * uy,
            root * uy * uz,
            root * ux * uz,
            0.5 * root * (ux * ux - uy * uy),
            0.5 * (3.0 * uz * uz - 1.0),
        ]
    )


def tile_terms(own_pos, other_pos, other_feat, pair_mask, listed, count):
    atoms = own_pos.shape[1]
    centres = 0.5 + jnp.arange(count).astype(jnp.float32)
    rel = other_pos[:, None, :] - own_pos[:, :, None]
    dist = jnp.sqrt(jnp.sum(rel * rel, axis=0) + 0.25)
    offset = dist[None] - centres[:, None, None]
    basis = jnp.exp(-0.5 * offset * offset)
    angular = harmonics(rel, dist)
    weight = pair_mask.astype(jnp.float32) * (1.0 / math.sqrt(listed * atoms))
    tiles = (basis[:, None] * angular[None] * weight[None, None]).reshape(count * 9, atoms, atoms)
    return jnp.einsum(
        "qij,cj->qci", tiles.astype(jnp.bfloat16), other_feat, preferred_element_type=jnp.float32
    )


def atom_energy(own_pos, others_pos, others_feat, masks, radial, readin, readout):
    count = radial.shape[0]
    width = others_feat.shape[1]
    atoms = own_pos.shape[1]
    listed = others_pos.shape[0]
    total = jnp.zeros((count * 9, width, atoms), jnp.float32)
    for slot in range(listed):
        total = total + tile_terms(
            own_pos, others_pos[slot], others_feat[slot], masks[slot], listed, count
        )
    proj = total.reshape(count, 9, width, atoms)
    message = jnp.sum(radial[:, None, :, None] * proj, axis=0)
    first = jnp.sum(message[1:4] * message[1:4], axis=0)
    second = jnp.sum(message[4:9] * message[4:9], axis=0)
    invariants = jnp.concatenate([message[0], first, second], axis=0)
    hidden = jax.nn.silu(jnp.dot(readin.T, invariants, precision=lax.Precision.HIGH))
    return jnp.dot(readout, hidden, precision=lax.Precision.HIGH)


def select_slots(table, chosen):
    slots = table.shape[0]
    hit = chosen[..., None] == jnp.arange(slots, dtype=chosen.dtype)
    hit = hit.reshape(hit.shape + (1,) * (table.ndim - 1))
    return jnp.sum(jnp.where(hit, table, jnp.zeros((), table.dtype)), axis=2)


def halo(grid):
    count_x = lax.axis_size("gx")
    count_y = lax.axis_size("gy")
    up_x = [(i, (i + 1) % count_x) for i in range(count_x)]
    down_x = [((i + 1) % count_x, i) for i in range(count_x)]
    up_y = [(i, (i + 1) % count_y) for i in range(count_y)]
    down_y = [((i + 1) % count_y, i) for i in range(count_y)]
    from_left_x = lax.ppermute(grid[2], "gx", up_x)
    from_right_x = lax.ppermute(grid[0], "gx", down_x)
    rows = jnp.stack([from_left_x, grid[1], from_right_x], axis=0)
    from_left_y = lax.ppermute(rows[:, 2], "gy", up_y)
    from_right_y = lax.ppermute(rows[:, 0], "gy", down_y)
    return jnp.stack([from_left_y, rows[:, 1], from_right_y], axis=1)


def place(parts):
    empty = jnp.zeros_like(parts[0:1])
    full = jnp.concatenate([parts[:4], empty, parts[4:]], axis=0)
    return full.reshape((3, 3) + parts.shape[1:])


def collect(grid):
    return jnp.stack([grid[1 + pair[0], 1 + pair[1]] for pair in OFFSETS], axis=0)


def local(
    positions, species, neighbours, pair_masks, send_lists, embedding, radial, readin, readout
):
    atoms = pair_masks.shape[2]
    blocks = positions.shape[1] // atoms
    kinds = embedding.shape[0]
    sends = send_lists.shape[3]
    own_pos = positions.reshape(3, blocks, atoms).transpose(1, 0, 2)
    own_kind = species.reshape(blocks, 1, atoms).astype(jnp.float32)
    payload = jnp.concatenate([own_pos, own_kind], axis=1)
    chosen = send_lists.reshape(8, sends)
    pick = (chosen[:, :, None] == jnp.arange(blocks)).astype(jnp.float32)
    outgoing = jnp.einsum("dgb,bra->dgra", pick, payload, precision=HIGHEST)
    incoming = collect(halo(place(outgoing))).reshape(8 * sends, 4, atoms)
    ghost_pos = incoming[:, :3]
    ghost_kind = incoming[:, 3]

    def features(kind):
        hit = kind[None, None, :] == jnp.arange(kinds).astype(kind.dtype)[:, None, None]
        return jnp.sum(jnp.where(hit, embedding[:, :, None], 0.0), axis=0)

    own_feats32 = features(species).reshape(-1, blocks, atoms).transpose(1, 0, 2)
    ghost_feats32 = (
        features(ghost_kind.reshape(-1)).reshape(-1, 8 * sends, atoms).transpose(1, 0, 2)
    )

    def energies_of(own_now, ghost_now):
        table_pos = jnp.concatenate([own_now, ghost_now], axis=0)
        table_feat = jnp.concatenate([own_feats32, ghost_feats32], axis=0)
        others_pos = select_slots(table_pos, neighbours)
        others_feat = select_slots(table_feat, neighbours).astype(jnp.bfloat16)
        return jnp.stack(
            [
                atom_energy(
                    own_now[block],
                    others_pos[block],
                    others_feat[block],
                    pair_masks[block],
                    radial,
                    readin,
                    readout,
                )
                for block in range(blocks)
            ]
        )

    energy, pullback = jax.vjp(energies_of, own_pos, ghost_pos)
    grad_own, grad_ghost = pullback(jnp.ones_like(energy))
    returned = collect(halo(place(grad_ghost.reshape(8, sends, 3, atoms))))
    back = jnp.einsum("dgb,dgca->bca", pick, returned, precision=HIGHEST)
    forces = -(grad_own + back)
    return (energy.reshape(blocks * atoms), forces.transpose(1, 0, 2).reshape(3, blocks * atoms))


def solution(mesh):
    placed = (
        P(None, ("gx", "gy")),
        P(("gx", "gy")),
        P(("gx", "gy"), None),
        P(("gx", "gy"), None, None, None),
        P("gx", "gy", None, None),
        P(),
        P(),
        P(),
        P(),
    )
    return jax.shard_map(
        local,
        mesh=mesh,
        in_specs=placed,
        out_specs=(P(("gx", "gy")), P(None, ("gx", "gy"))),
        check_vma=False,
    )
```

```python
import math

import jax
import jax.numpy as jnp
from jax import lax
from jax.sharding import PartitionSpec as P

OFFSETS = ((-1, -1), (-1, 0), (-1, 1), (0, -1), (0, 1), (1, -1), (1, 0), (1, 1))
HIGHEST = lax.Precision.HIGHEST


def harmonics(rel, dist):
    ux = rel[0] / dist
    uy = rel[1] / dist
    uz = rel[2] / dist
    root = math.sqrt(3.0)
    return jnp.stack(
        [
            jnp.ones_like(ux),
            ux,
            uy,
            uz,
            root * ux * uy,
            root * uy * uz,
            root * ux * uz,
            0.5 * root * (ux * ux - uy * uy),
            0.5 * (3.0 * uz * uz - 1.0),
        ]
    )


def tile_terms(own_pos, other_pos, other_feat, pair_mask, listed, count):
    atoms = own_pos.shape[1]
    centres = 0.5 + jnp.arange(count).astype(jnp.float32)
    rel = other_pos[:, None, :] - own_pos[:, :, None]
    dist = jnp.sqrt(jnp.sum(rel * rel, axis=0) + 0.25)
    offset = dist[None] - centres[:, None, None]
    basis = jnp.exp(-0.5 * offset * offset)
    angular = harmonics(rel, dist)
    weight = pair_mask.astype(jnp.float32) * (1.0 / math.sqrt(listed * atoms))
    tiles = (basis[:, None] * angular[None] * weight[None, None]).reshape(count * 9, atoms, atoms)
    return jnp.einsum(
        "qij,cj->qci", tiles.astype(jnp.bfloat16), other_feat, preferred_element_type=jnp.float32
    )


def atom_energy(own_pos, others_pos, others_feat, masks, radial, readin, readout):
    count = radial.shape[0]
    width = others_feat.shape[1]
    atoms = own_pos.shape[1]
    listed = others_pos.shape[0]
    total = jnp.zeros((count * 9, width, atoms), jnp.float32)
    for slot in range(listed):
        total = total + tile_terms(
            own_pos, others_pos[slot], others_feat[slot], masks[slot], listed, count
        )
    proj = total.reshape(count, 9, width, atoms)
    message = jnp.sum(radial[:, None, :, None] * proj, axis=0)
    first = jnp.sum(message[1:4] * message[1:4], axis=0)
    second = jnp.sum(message[4:9] * message[4:9], axis=0)
    invariants = jnp.concatenate([message[0], first, second], axis=0)
    hidden = jax.nn.silu(jnp.dot(readin.T, invariants, precision=lax.Precision.HIGH))
    return jnp.dot(readout, hidden, precision=lax.Precision.HIGH)


def select_slots(table, chosen):
    slots = table.shape[0]
    hit = chosen[..., None] == jnp.arange(slots, dtype=chosen.dtype)
    hit = hit.reshape(hit.shape + (1,) * (table.ndim - 1))
    return jnp.sum(jnp.where(hit, table, jnp.zeros((), table.dtype)), axis=2)


def halo(grid):
    count_x = lax.axis_size("gx")
    count_y = lax.axis_size("gy")
    up_x = [(i, (i + 1) % count_x) for i in range(count_x)]
    down_x = [((i + 1) % count_x, i) for i in range(count_x)]
    up_y = [(i, (i + 1) % count_y) for i in range(count_y)]
    down_y = [((i + 1) % count_y, i) for i in range(count_y)]
    from_left_x = lax.ppermute(grid[2], "gx", up_x)
    from_right_x = lax.ppermute(grid[0], "gx", down_x)
    rows = jnp.stack([from_left_x, grid[1], from_right_x], axis=0)
    from_left_y = lax.ppermute(rows[:, 2], "gy", up_y)
    from_right_y = lax.ppermute(rows[:, 0], "gy", down_y)
    return jnp.stack([from_left_y, rows[:, 1], from_right_y], axis=1)


def place(parts):
    empty = jnp.zeros_like(parts[0:1])
    full = jnp.concatenate([parts[:4], empty, parts[4:]], axis=0)
    return full.reshape((3, 3) + parts.shape[1:])


def collect(grid):
    return jnp.stack([grid[1 + pair[0], 1 + pair[1]] for pair in OFFSETS], axis=0)


def local(
    positions, species, neighbours, pair_masks, send_lists, embedding, radial, readin, readout
):
    atoms = pair_masks.shape[2]
    blocks = positions.shape[1] // atoms
    kinds = embedding.shape[0]
    sends = send_lists.shape[3]
    own_pos = positions.reshape(3, blocks, atoms).transpose(1, 0, 2)
    own_kind = species.reshape(blocks, 1, atoms).astype(jnp.float32)
    payload = jnp.concatenate([own_pos, own_kind], axis=1)
    chosen = send_lists.reshape(8, sends)
    pick = (chosen[:, :, None] == jnp.arange(blocks)).astype(jnp.float32)
    outgoing = jnp.sum(jnp.where(pick[:, :, :, None, None] > 0, payload[None, None], 0.0), axis=2)
    incoming = collect(halo(place(outgoing))).reshape(8 * sends, 4, atoms)
    ghost_pos = incoming[:, :3]
    ghost_kind = incoming[:, 3]

    def features(kind):
        onehot = (kind[None, :] == jnp.arange(kinds).astype(kind.dtype)[:, None]).astype(jnp.float32)
        return jnp.dot(embedding.T, onehot, precision=HIGHEST)

    own_feats32 = features(species).reshape(-1, blocks, atoms).transpose(1, 0, 2)
    ghost_feats32 = (
        features(ghost_kind.reshape(-1)).reshape(-1, 8 * sends, atoms).transpose(1, 0, 2)
    )

    def energies_of(own_now, ghost_now):
        table_pos = jnp.concatenate([own_now, ghost_now], axis=0)
        table_feat = jnp.concatenate([own_feats32, ghost_feats32], axis=0)
        others_pos = select_slots(table_pos, neighbours)
        others_feat = select_slots(table_feat, neighbours).astype(jnp.bfloat16)
        return jnp.stack(
            [
                atom_energy(
                    own_now[block],
                    others_pos[block],
                    others_feat[block],
                    pair_masks[block],
                    radial,
                    readin,
                    readout,
                )
                for block in range(blocks)
            ]
        )

    energy, pullback = jax.vjp(energies_of, own_pos, ghost_pos)
    grad_own, grad_ghost = pullback(jnp.ones_like(energy))
    returned = collect(halo(place(grad_ghost.reshape(8, sends, 3, atoms))))
    back = jnp.einsum("dgb,dgca->bca", pick, returned, precision=HIGHEST)
    forces = -(grad_own + back)
    return (energy.reshape(blocks * atoms), forces.transpose(1, 0, 2).reshape(3, blocks * atoms))


def solution(mesh):
    placed = (
        P(None, ("gx", "gy")),
        P(("gx", "gy")),
        P(("gx", "gy"), None),
        P(("gx", "gy"), None, None, None),
        P("gx", "gy", None, None),
        P(),
        P(),
        P(),
        P(),
    )
    return jax.shard_map(
        local,
        mesh=mesh,
        in_specs=placed,
        out_specs=(P(("gx", "gy")), P(None, ("gx", "gy"))),
        check_vma=False,
    )
```

```python
import math

import jax
import jax.numpy as jnp
from jax import lax
from jax.sharding import PartitionSpec as P

OFFSETS = ((-1, -1), (-1, 0), (-1, 1), (0, -1), (0, 1), (1, -1), (1, 0), (1, 1))
HIGHEST = lax.Precision.HIGHEST


def harmonics(rel, dist):
    ux = rel[0] / dist
    uy = rel[1] / dist
    uz = rel[2] / dist
    root = math.sqrt(3.0)
    return jnp.stack(
        [
            jnp.ones_like(ux),
            ux,
            uy,
            uz,
            root * ux * uy,
            root * uy * uz,
            root * ux * uz,
            0.5 * root * (ux * ux - uy * uy),
            0.5 * (3.0 * uz * uz - 1.0),
        ]
    )


def tile_terms(own_pos, other_pos, other_feat, pair_mask, listed, count):
    atoms = own_pos.shape[1]
    centres = 0.5 + jnp.arange(count).astype(jnp.float32)
    rel = other_pos[:, None, :] - own_pos[:, :, None]
    dist = jnp.sqrt(jnp.sum(rel * rel, axis=0) + 0.25)
    offset = dist[None] - centres[:, None, None]
    basis = jnp.exp(-0.5 * offset * offset)
    angular = harmonics(rel, dist)
    weight = pair_mask.astype(jnp.float32) * (1.0 / math.sqrt(listed * atoms))
    tiles = (basis[:, None] * angular[None] * weight[None, None]).reshape(count * 9, atoms, atoms)
    return jnp.einsum(
        "qij,cj->qci", tiles.astype(jnp.bfloat16), other_feat, preferred_element_type=jnp.float32
    )


def atom_energy(own_pos, others_pos, others_feat, masks, radial, readin, readout):
    count = radial.shape[0]
    width = others_feat.shape[1]
    atoms = own_pos.shape[1]
    listed = others_pos.shape[0]
    total = jnp.zeros((count * 9, width, atoms), jnp.float32)
    for slot in range(listed):
        total = total + tile_terms(
            own_pos, others_pos[slot], others_feat[slot], masks[slot], listed, count
        )
    proj = total.reshape(count, 9, width, atoms)
    message = jnp.sum(radial[:, None, :, None] * proj, axis=0)
    first = jnp.sum(message[1:4] * message[1:4], axis=0)
    second = jnp.sum(message[4:9] * message[4:9], axis=0)
    invariants = jnp.concatenate([message[0], first, second], axis=0)
    hidden = jax.nn.silu(jnp.dot(readin.T, invariants, precision=lax.Precision.HIGH))
    return jnp.dot(readout, hidden, precision=lax.Precision.HIGH)


def select_slots(table, chosen):
    slots = table.shape[0]
    hit = chosen[..., None] == jnp.arange(slots, dtype=chosen.dtype)
    hit = hit.reshape(hit.shape + (1,) * (table.ndim - 1))
    return jnp.sum(jnp.where(hit, table, jnp.zeros((), table.dtype)), axis=2)


def halo(grid):
    count_x = lax.axis_size("gx")
    count_y = lax.axis_size("gy")
    up_x = [(i, (i + 1) % count_x) for i in range(count_x)]
    down_x = [((i + 1) % count_x, i) for i in range(count_x)]
    up_y = [(i, (i + 1) % count_y) for i in range(count_y)]
    down_y = [((i + 1) % count_y, i) for i in range(count_y)]
    from_left_x = lax.ppermute(grid[2], "gx", up_x)
    from_right_x = lax.ppermute(grid[0], "gx", down_x)
    rows = jnp.stack([from_left_x, grid[1], from_right_x], axis=0)
    from_left_y = lax.ppermute(rows[:, 2], "gy", up_y)
    from_right_y = lax.ppermute(rows[:, 0], "gy", down_y)
    return jnp.stack([from_left_y, rows[:, 1], from_right_y], axis=1)


def place(parts):
    empty = jnp.zeros_like(parts[0:1])
    full = jnp.concatenate([parts[:4], empty, parts[4:]], axis=0)
    return full.reshape((3, 3) + parts.shape[1:])


def collect(grid):
    return jnp.stack([grid[1 + pair[0], 1 + pair[1]] for pair in OFFSETS], axis=0)


def local(
    positions, species, neighbours, pair_masks, send_lists, embedding, radial, readin, readout
):
    atoms = pair_masks.shape[2]
    blocks = positions.shape[1] // atoms
    kinds = embedding.shape[0]
    sends = send_lists.shape[3]
    own_pos = positions.reshape(3, blocks, atoms).transpose(1, 0, 2)
    own_kind = species.reshape(blocks, 1, atoms).astype(jnp.float32)
    payload = jnp.concatenate([own_pos, own_kind], axis=1)
    chosen = send_lists.reshape(8, sends)
    pick = (chosen[:, :, None] == jnp.arange(blocks)).astype(jnp.float32)
    outgoing = jnp.einsum("dgb,bra->dgra", pick, payload, precision=HIGHEST)
    incoming = collect(halo(place(outgoing))).reshape(8 * sends, 4, atoms)
    ghost_pos = incoming[:, :3]
    ghost_kind = incoming[:, 3]

    def features(kind):
        onehot = (kind[None, :] == jnp.arange(kinds).astype(kind.dtype)[:, None]).astype(jnp.float32)
        return jnp.dot(embedding.T, onehot, precision=HIGHEST)

    own_feats32 = features(species).reshape(-1, blocks, atoms).transpose(1, 0, 2)
    ghost_feats32 = (
        features(ghost_kind.reshape(-1)).reshape(-1, 8 * sends, atoms).transpose(1, 0, 2)
    )

    def energies_of(own_now, ghost_now):
        table_pos = jnp.concatenate([own_now, ghost_now], axis=0)
        table_feat = jnp.concatenate([own_feats32, ghost_feats32], axis=0)
        others_pos = select_slots(table_pos, neighbours)
        others_feat = select_slots(table_feat, neighbours).astype(jnp.bfloat16)
        return jnp.stack(
            [
                atom_energy(
                    own_now[block],
                    others_pos[block],
                    others_feat[block],
                    pair_masks[block],
                    radial,
                    readin,
                    readout,
                )
                for block in range(blocks)
            ]
        )

    energy, pullback = jax.vjp(energies_of, own_pos, ghost_pos)
    grad_own, grad_ghost = pullback(jnp.ones_like(energy))
    returned = collect(halo(place(grad_ghost.reshape(8, sends, 3, atoms))))
    back = jnp.sum(jnp.where(pick[:, :, :, None, None] > 0, returned[:, :, None], 0.0), axis=(0, 1))
    forces = -(grad_own + back)
    return (energy.reshape(blocks * atoms), forces.transpose(1, 0, 2).reshape(3, blocks * atoms))


def solution(mesh):
    placed = (
        P(None, ("gx", "gy")),
        P(("gx", "gy")),
        P(("gx", "gy"), None),
        P(("gx", "gy"), None, None, None),
        P("gx", "gy", None, None),
        P(),
        P(),
        P(),
        P(),
    )
    return jax.shard_map(
        local,
        mesh=mesh,
        in_specs=placed,
        out_specs=(P(("gx", "gy")), P(None, ("gx", "gy"))),
        check_vma=False,
    )
```
